256 devices in a mesh: cfg: 2 (over core), req: 8 (over z), seq: 16 (over y, x).
Axes of the slice: x: 4, y: 4, z: 8, core: 2. Of those that a mesh axis runs over, the one named last changes fastest.
Arguments:
- img_hidden: bfloat16 [2, 16, 512, 1536], P('cfg', 'req', 'seq'), may hold values from -6 to 6
- txt_hidden: bfloat16 [2, 16, 160, 1536], P('cfg', 'req', 'seq'), may hold values from -6 to 6
- text_len: int32 [2, 16], P('cfg'), may hold values from 1 to 154, as said below
- pooled: float32 [2, 16, 1536], P('cfg'), may hold values from -6 to 6
- timestep: int32 [16], replicated, may hold values from 0 to 27
- latent: float32 [16, 512, 64], P('req', 'seq', 'cfg'), may hold values from -24 to 24
- mod_weight: bfloat16 [1536, 15360], P(None, ('req', 'seq')), may hold values from -0.15625 to 0.15625
- mod_bias: float32 [15360], P(('req', 'seq')), may hold values from -2 to 2
- img_qkv: bfloat16 [1536, 3, 1536], P(None, None, 'req'), may hold values from -2.5 to 2.5
- txt_kv: bfloat16 [1536, 2, 1536], P(None, None, 'req'), may hold values from -0.15625 to 0.15625
- out_weight: bfloat16 [1536, 1536], P('req'), may hold values from -0.15625 to 0.15625
- fc_in: bfloat16 [1536, 6144], P(None, 'seq'), may hold values from -0.15625 to 0.15625
- fc_out: bfloat16 [6144, 1536], P('seq'), may hold values from -0.078125 to 0.078125
- final_weight: bfloat16 [1536, 64], replicated, may hold values from -0.15625 to 0.15625
Outputs:
- velocity: float32 [16, 512, 64], P('req', 'seq', 'cfg')
- next_latent: float32 [16, 512, 64], P('req', 'seq', 'cfg')
- latent_norm: float32 [16], P('req')
- latent_peak: float32 [16], P('req')
The draws below stay inside these ranges and needn't reach their ends.
Inputs may be any that keep to these rules, and one draw needn't show every extreme that they name: Text slots from text_len to 159 of a request are padding; every draw has a request of length 154 and one of length 1.
All inputs are finite; a program needn't handle non-finite values.
Results may differ from the reference program's by a relative error of at most 0.015.
Values may be sent and summed in bfloat16 or wider, within the bound.
No kernel may reach another device: no remote copies, remote signals or barrier semaphores. Data moves between devices by JAX's collectives and lax.ppermute only.
A program may use at most 64 MiB of HBM per device.

```python
import math
import jax
import jax.numpy as jnp
from jax import lax

D = 1536
HEADS = 24
HD = 64
FF = 6144
PATCHC = 64
TXT = 154
IMG = 512
STEPS = 28
REQS = 16
TXTP = 160
N_SEQ = 16


def draw_text_len(key, part):
    lengths = jax.random.randint(key, (2 * REQS,), 1, TXT + 1)
    chosen = jax.random.randint(jax.random.fold_in(key, 7), (), 0, 2 * REQS)
    second = (chosen + 1 + jax.random.randint(jax.random.fold_in(key, 11), (), 0, 2 * REQS - 1)) % (2 * REQS)
    positions = jnp.arange(2 * REQS)
    lengths = jnp.where(positions == chosen, TXT, lengths)
    lengths = jnp.where(positions == second, 1, lengths)
    return lengths.reshape(2, REQS).astype(jnp.int32)


def draw_latent(key, part):
    position = jnp.arange(IMG, dtype=jnp.float32) / max(IMG - 1, 1)
    ramp_scale = 1.0 + 2.0 * position
    row_scale = ramp_scale[None, :, None] * jnp.exp(jax.random.uniform(jax.random.fold_in(key, 1), (REQS, IMG, 1), minval=0.0, maxval=math.log(4.0)))
    samples = jnp.clip(jax.random.normal(key, (REQS, IMG, PATCHC)), -5.0, 5.0)
    return (samples * row_scale * 0.4).astype(jnp.float32)


def draw_img_qkv(key, part):
    weights = jnp.clip(jax.random.normal(key, (D, 3, D)), -6.0, 6.0) * D ** (-0.5)
    return jnp.clip(weights, -2.5, 2.5).astype(jnp.bfloat16)


def with_ends(array, rng, smallest, top_value):
    spot = [jax.random.randint(jax.random.fold_in(rng, axis), (), 0, length) for axis, length in enumerate(array.shape)]
    longest = array.shape.index(max(array.shape))
    neighbour = spot[:longest] + [(spot[longest] + 1) % array.shape[longest]] + spot[longest + 1:]
    return array.at[tuple(spot)].set(smallest).at[tuple(neighbour)].set(top_value)


def block_scale(stream_key, extent, cuts, least, largest):
    def one(dim, blocks):
        heights = jax.random.uniform(jax.random.fold_in(jax.random.fold_in(stream_key, 6), dim), (blocks,), jnp.float32, least / len(cuts), largest / len(cuts))
        return jnp.repeat(jnp.exp(heights), extent[dim] // blocks).reshape((-1,) + (1,) * (len(extent) - dim - 1))

    factor_of = one(*cuts[0])
    for cut in cuts[1:]:
        factor_of = factor_of * one(*cut)
    return factor_of


def gaussian(key, extent, deviation, limit, shards=(), kind=jnp.bfloat16):
    drawn = jax.random.normal(key, extent, jnp.float32) * deviation
    if len(shards) > 0:
        drawn = block_scale(key, extent, shards, -0.22, 0.18) * drawn
    return jnp.clip(drawn, min=-limit, max=limit).astype(kind)


def setup_inputs(seed: int = 0) -> dict:
    seeds = jax.random.split(jax.random.key(seed), 15)
    img_hidden = gaussian(seeds[0], (2, REQS, IMG, D), 1.0, 6.0, ((0, 2), (1, 8), (2, 16)))
    txt_hidden = gaussian(seeds[1], (2, REQS, TXTP, D), 1.0, 6.0, ((0, 2), (1, 8), (2, 16)))
    text_len = draw_text_len(jax.random.fold_in(seeds[14], 71), 0)
    pooled = gaussian(seeds[3], (2, REQS, D), 1.0, 6.0, ((0, 2),), jnp.float32)
    timestep = with_ends(jax.random.randint(seeds[4], (REQS,), 0, STEPS), jax.random.fold_in(seeds[4], 1), 0, STEPS - 1).astype(jnp.int32)
    latent = draw_latent(jax.random.fold_in(seeds[14], 71), 0)
    mod_weight = gaussian(seeds[6], (D, 10 * D), D ** -0.5, 0.15625, ((1, 128),))
    mod_bias = gaussian(seeds[7], (10 * D,), 0.3, 2.0, ((0, 128),), jnp.float32)
    img_qkv = draw_img_qkv(jax.random.fold_in(seeds[14], 71), 0)
    txt_kv = gaussian(seeds[9], (D, 2, D), D ** -0.5, 0.15625, ((2, 8),))
    out_weight = gaussian(seeds[10], (D, D), D ** -0.5, 0.15625, ((0, 8),))
    fc_in = gaussian(seeds[11], (D, FF), D ** -0.5, 0.15625, ((1, 16),))
    fc_out = gaussian(seeds[12], (FF, D), FF ** -0.5, 0.078125, ((0, 16),))
    final_weight = gaussian(seeds[13], (D, PATCHC), D ** -0.5, 0.15625)
    return dict(img_hidden=img_hidden, txt_hidden=txt_hidden, text_len=text_len, pooled=pooled, timestep=timestep, latent=latent, mod_weight=mod_weight, mod_bias=mod_bias, img_qkv=img_qkv, txt_kv=txt_kv, out_weight=out_weight, fc_in=fc_in, fc_out=fc_out, final_weight=final_weight)


SIGMA_SHIFT = 3.0
GUIDANCE = 5.0
EPSILON = 1e-06
MASKED_SCORE = -1e+30

def shifted(fraction):
    return SIGMA_SHIFT * fraction / (1.0 + (SIGMA_SHIFT - 1.0) * fraction)

def plan(timestep):
    position = timestep.astype(jnp.float32)
    return (shifted(1.0 - position / STEPS), shifted(1.0 - (position + 1.0) / STEPS))

def time_features(sigma):
    half_width = D // 2
    frequency = jnp.exp(-math.log(10000.0) * jnp.arange(half_width, dtype=jnp.float32) / half_width)
    angles = (1000.0 * sigma)[:, None] * frequency[None, :]
    return jnp.concatenate([jnp.cos(angles), jnp.sin(angles)], axis=1)

def layer_norm(values):
    average = lax.optimization_barrier(jnp.mean(values, axis=-1, keepdims=True))
    centred = values - average
    spread = lax.optimization_barrier(jnp.mean(centred * centred, axis=-1, keepdims=True))
    return centred * lax.rsqrt(spread + EPSILON)

def attention(queries, key_rows, value_rows, live_keys):
    query_count = queries.shape[0]
    head_count = queries.shape[1]
    block_rows = min(512, query_count)
    scale_factor = HD ** (-0.5)

    def one_block(query_block):
        scores = jnp.einsum('qhd,khd->hqk', query_block.astype(jnp.float32), key_rows.astype(jnp.float32)) * scale_factor
        scores = jnp.where(live_keys[None, None, :], scores, MASKED_SCORE)
        highest = lax.optimization_barrier(jnp.max(scores, axis=-1, keepdims=True))
        exp_scores = jnp.exp(scores - highest)
        weights = (exp_scores / lax.optimization_barrier(jnp.sum(exp_scores, axis=-1, keepdims=True))).astype(jnp.bfloat16)
        mixture = jnp.einsum('hqk,khd->qhd', weights.astype(jnp.float32), value_rows.astype(jnp.float32))
        return mixture.astype(jnp.bfloat16)
    blocks = queries.reshape(query_count // block_rows, block_rows, head_count, HD)
    return lax.map(one_block, blocks).reshape(query_count, head_count * HD)

def request_velocity(img_rows, txt_rows, text_count, modulation, img_qkv, txt_kv, out_weight, fc_in, fc_out, final_weight):
    mod_parts = modulation.reshape(10, D)
    shift_attn, scale_attn, gate_attn = (mod_parts[0], mod_parts[1], mod_parts[2])
    shift_mlp, scale_mlp, gate_mlp = (mod_parts[3], mod_parts[4], mod_parts[5])
    shift_text, scale_text = (mod_parts[6], mod_parts[7])
    scale_final, shift_final = (mod_parts[8], mod_parts[9])
    img_float = img_rows.astype(jnp.float32)
    img_in = (layer_norm(img_float) * (1.0 + scale_attn) + shift_attn).astype(jnp.bfloat16)
    txt_in = (layer_norm(txt_rows.astype(jnp.float32)) * (1.0 + scale_text) + shift_text).astype(jnp.bfloat16)
    queries = jnp.dot(img_in, img_qkv[:, 0, :], preferred_element_type=jnp.float32).astype(jnp.bfloat16)
    key_rows = jnp.concatenate([jnp.dot(img_in, img_qkv[:, 1, :], preferred_element_type=jnp.float32).astype(jnp.bfloat16), jnp.dot(txt_in, txt_kv[:, 0, :], preferred_element_type=jnp.float32).astype(jnp.bfloat16)], axis=0)
    value_rows = jnp.concatenate([jnp.dot(img_in, img_qkv[:, 2, :], preferred_element_type=jnp.float32).astype(jnp.bfloat16), jnp.dot(txt_in, txt_kv[:, 1, :], preferred_element_type=jnp.float32).astype(jnp.bfloat16)], axis=0)
    live_keys = jnp.arange(IMG + TXTP, dtype=jnp.int32) < IMG + text_count
    attended = attention(queries.reshape(IMG, HEADS, HD), key_rows.reshape(IMG + TXTP, HEADS, HD), value_rows.reshape(IMG + TXTP, HEADS, HD), live_keys)
    img_mid = img_float + gate_attn * jnp.dot(attended, out_weight, preferred_element_type=jnp.float32)
    mlp_in = (layer_norm(img_mid) * (1.0 + scale_mlp) + shift_mlp).astype(jnp.bfloat16)
    hidden = jax.nn.gelu(jnp.dot(mlp_in, fc_in, preferred_element_type=jnp.float32), approximate=True).astype(jnp.bfloat16)
    share_width = FF // N_SEQ

    def add_share(running, shard_index):
        offset = shard_index * share_width
        partial_value = jnp.dot(lax.dynamic_slice_in_dim(hidden, offset, share_width, 1), lax.dynamic_slice_in_dim(fc_out, offset, share_width, 0), preferred_element_type=jnp.float32)
        rounded = lax.optimization_barrier(partial_value.astype(jnp.bfloat16))
        return (running + rounded.astype(jnp.float32), None)
    mlp_out = lax.scan(add_share, jnp.zeros((IMG, D), jnp.float32), jnp.arange(N_SEQ, dtype=jnp.int32))[0]
    img_out = img_mid + gate_mlp * mlp_out
    final_in = (layer_norm(img_out) * (1.0 + scale_final) + shift_final).astype(jnp.bfloat16)
    return jnp.dot(final_in, final_weight, preferred_element_type=jnp.float32)

def reference(img_hidden, txt_hidden, text_len, pooled, timestep, latent, mod_weight, mod_bias, img_qkv, txt_kv, out_weight, fc_in, fc_out, final_weight):
    current, upcoming = plan(timestep)
    features = time_features(current)
    velocities = []
    for half_index in range(2):
        activated = jax.nn.silu(pooled[half_index] + features).astype(jnp.bfloat16)
        modulation = jnp.dot(activated, mod_weight, preferred_element_type=jnp.float32) + mod_bias

        def one_request(operands):
            return request_velocity(operands[0], operands[1], operands[2], operands[3], img_qkv, txt_kv, out_weight, fc_in, fc_out, final_weight)
        velocities.append(lax.map(one_request, (img_hidden[half_index], txt_hidden[half_index], text_len[half_index], modulation)))
    guided = velocities[1] + GUIDANCE * (velocities[0] - velocities[1])
    next_latent = latent + (upcoming - current)[:, None, None] * guided
    latent_norm = jnp.sqrt(lax.optimization_barrier(jnp.mean(next_latent * next_latent, axis=(1, 2))))
    latent_peak = lax.optimization_barrier(jnp.max(jnp.abs(next_latent), axis=(1, 2)))
    return (guided, next_latent, latent_norm, latent_peak)
```

```python
import math

import jax
import jax.numpy as jnp
from jax import lax
from jax.sharding import PartitionSpec as P

D = 1536
HD = 64
PATCHC = 64
IMG = 512
STEPS = 28


SIGMA_SHIFT = 3.0
GUIDANCE = 5.0
EPSILON = 1e-06
MASKED_SCORE = -1e30


def xor_pairs(axis, distance):
    return [(source, source ^ distance) for source in range(lax.axis_size(axis))]


def shifted(fraction):
    return SIGMA_SHIFT * fraction / (1.0 + (SIGMA_SHIFT - 1.0) * fraction)


def plan(timestep):
    position = timestep.astype(jnp.float32)
    return (shifted(1.0 - position / STEPS), shifted(1.0 - (position + 1.0) / STEPS))


def time_features(sigma):
    half_width = D // 2
    frequency = jnp.exp(-math.log(10000.0) * jnp.arange(half_width, dtype=jnp.float32) / half_width)
    angles = (1000.0 * sigma)[:, None] * frequency[None, :]
    return jnp.concatenate([jnp.cos(angles), jnp.sin(angles)], axis=1)


def layer_norm(values):
    average = jnp.mean(values, axis=-1, keepdims=True)
    centred = values - average
    spread = jnp.mean(centred * centred, axis=-1, keepdims=True)
    return centred * lax.rsqrt(spread + EPSILON)


def gather_by_a2a(value, axis):
    count = lax.axis_size(axis)
    copies = jnp.broadcast_to(value[None], (count,) + value.shape)
    return lax.all_to_all(copies, axis, 0, 0, tiled=True)


def attention(queries, key_rows, value_rows, live_keys):
    scale_factor = HD ** (-0.5)
    scores = (
        jnp.einsum("qhd,khd->hqk", queries, key_rows, preferred_element_type=jnp.float32)
        * scale_factor
    )
    scores = jnp.where(live_keys[None, None, :], scores, MASKED_SCORE)
    highest = jnp.max(scores, axis=-1, keepdims=True)
    exp_scores = jnp.exp(scores - highest)
    weights = (exp_scores / jnp.sum(exp_scores, axis=-1, keepdims=True)).astype(jnp.bfloat16)
    mixture = jnp.einsum("hqk,khd->qhd", weights, value_rows, preferred_element_type=jnp.float32)
    return mixture.astype(jnp.bfloat16)


def on_device(
    img_hidden,
    txt_hidden,
    text_len,
    pooled,
    timestep,
    latent,
    mod_weight,
    mod_bias,
    img_qkv,
    txt_kv,
    out_weight,
    fc_in,
    fc_out,
    final_weight,
):
    group_size = img_hidden.shape[1]
    req_count = lax.axis_size("req")
    seq_count = lax.axis_size("seq")
    current, upcoming = plan(timestep)
    activated = jax.nn.silu(pooled[0] + time_features(current)).astype(jnp.bfloat16)
    columns = jnp.dot(activated, mod_weight, preferred_element_type=jnp.float32) + mod_bias
    block_width = columns.shape[1]
    mine = lax.all_to_all(
        columns.reshape(req_count, group_size, block_width), "req", 0, 0, tiled=True
    )
    every = gather_by_a2a(mine, "seq")
    every = every.transpose(2, 1, 0, 3).reshape(group_size, req_count * seq_count * block_width)
    modulation = every.reshape(group_size, 10, 1, D)
    shift_attn, scale_attn, gate_attn = (modulation[:, 0], modulation[:, 1], modulation[:, 2])
    shift_mlp, scale_mlp, gate_mlp = (modulation[:, 3], modulation[:, 4], modulation[:, 5])
    shift_text, scale_text = (modulation[:, 6], modulation[:, 7])
    scale_final, shift_final = (modulation[:, 8], modulation[:, 9])
    img_float = img_hidden[0].astype(jnp.float32)
    img_in = (layer_norm(img_float) * (1.0 + scale_attn) + shift_attn).astype(jnp.bfloat16)
    txt_in = (
        layer_norm(txt_hidden[0].astype(jnp.float32)) * (1.0 + scale_text) + shift_text
    ).astype(jnp.bfloat16)
    row_count = img_in.shape[1]
    text_block = txt_in.shape[1]
    both = gather_by_a2a(jnp.concatenate([img_in, txt_in], axis=1), "req")
    both = both.reshape(req_count * group_size, row_count + text_block, D)
    head_width = img_qkv.shape[2]
    local_heads = head_width // HD
    qkv_columns = img_qkv.reshape(D, 3 * head_width)
    kv_columns = txt_kv.reshape(D, 2 * head_width)
    proj_img = jnp.einsum(
        "rnd,dc->rnc", both[:, :row_count], qkv_columns, preferred_element_type=jnp.float32
    ).astype(jnp.bfloat16)
    proj_txt = jnp.einsum(
        "rnd,dc->rnc", both[:, row_count:], kv_columns, preferred_element_type=jnp.float32
    ).astype(jnp.bfloat16)
    request_count = proj_img.shape[0]
    img_size = row_count * 3 * head_width
    packed = jnp.concatenate(
        [proj_img.reshape(request_count, img_size), proj_txt.reshape(request_count, -1)], axis=1
    )
    own = lax.all_to_all(packed, "seq", 0, 0, tiled=True)
    image_rows = seq_count * row_count
    text_rows = seq_count * text_block
    own_img = own[:, :img_size].reshape(image_rows, 3 * head_width)
    own_txt = own[:, img_size:].reshape(text_rows, 2 * head_width)
    queries = own_img[:, :head_width]
    key_rows = jnp.concatenate([own_img[:, head_width : 2 * head_width], own_txt[:, :head_width]], 0)
    value_rows = jnp.concatenate([own_img[:, 2 * head_width :], own_txt[:, head_width:]], 0)
    text_count = lax.dynamic_index_in_dim(text_len[0], lax.axis_index("seq"), 0, False)
    total_keys = image_rows + text_rows
    live_keys = jnp.arange(total_keys, dtype=jnp.int32) < image_rows + text_count
    attended = attention(
        queries.reshape(image_rows, local_heads, HD),
        key_rows.reshape(total_keys, local_heads, HD),
        value_rows.reshape(total_keys, local_heads, HD),
        live_keys,
    ).reshape(seq_count, row_count, head_width)
    attended_rows = lax.all_to_all(attended, "seq", 0, 0, tiled=True)
    partial = jnp.einsum(
        "rnk,kd->rnd", attended_rows, out_weight, preferred_element_type=jnp.float32
    ).astype(jnp.bfloat16)
    head_terms = lax.all_to_all(
        partial.reshape(req_count, group_size, row_count, D), "req", 0, 0, tiled=True
    )
    attn_out = jnp.sum(head_terms.astype(jnp.float32), axis=0)
    img_mid = img_float + gate_attn * attn_out
    mlp_in = (layer_norm(img_mid) * (1.0 + scale_mlp) + shift_mlp).astype(jnp.bfloat16)
    all_rows = gather_by_a2a(mlp_in, "seq")
    raised = jnp.einsum("srnd,df->srnf", all_rows, fc_in, preferred_element_type=jnp.float32)
    hidden = jax.nn.gelu(raised, approximate=True).astype(jnp.bfloat16)
    mlp_terms = jnp.einsum(
        "srnf,fd->srnd", hidden, fc_out, preferred_element_type=jnp.float32
    ).astype(jnp.bfloat16)
    block_terms = lax.all_to_all(mlp_terms, "seq", 0, 0, tiled=True)
    mlp_out = jnp.sum(block_terms.astype(jnp.float32), axis=0)
    img_out = img_mid + gate_mlp * mlp_out
    final_in = (layer_norm(img_out) * (1.0 + scale_final) + shift_final).astype(jnp.bfloat16)
    own_velocity = jnp.einsum(
        "rnd,dc->rnc", final_in, final_weight, preferred_element_type=jnp.float32
    )
    half_values = latent.shape[2]
    half_index = lax.axis_index("cfg")
    kept_velocity = lax.dynamic_slice_in_dim(own_velocity, half_index * half_values, half_values, 2)
    sent_velocity = lax.dynamic_slice_in_dim(
        own_velocity, (1 - half_index) * half_values, half_values, 2
    )
    other_velocity = lax.ppermute(sent_velocity, "cfg", xor_pairs("cfg", 1))
    cond_first = half_index == 0
    conditional = jnp.where(cond_first, kept_velocity, other_velocity)
    unconditional = jnp.where(cond_first, other_velocity, kept_velocity)
    guided = unconditional + GUIDANCE * (conditional - unconditional)
    offset = lax.axis_index("req") * group_size
    step_size = lax.dynamic_slice_in_dim(upcoming - current, offset, group_size, 0)
    next_latent = latent + step_size[:, None, None] * guided
    squares = jnp.sum(next_latent * next_latent, axis=(1, 2))
    largest = jnp.max(jnp.abs(next_latent), axis=(1, 2))
    for axis, distance in (("seq", 1), ("seq", 2), ("seq", 4), ("seq", 8), ("cfg", 1)):
        if distance >= lax.axis_size(axis):
            continue
        stats = lax.ppermute(jnp.stack([squares, largest]), axis, xor_pairs(axis, distance))
        squares = squares + stats[0]
        largest = jnp.maximum(largest, stats[1])
    latent_norm = jnp.sqrt(squares / (IMG * PATCHC))
    return (guided, next_latent, latent_norm, largest)


def solution(mesh):
    placed = (
        P("cfg", "req", "seq", None),
        P("cfg", "req", "seq", None),
        P("cfg", None),
        P("cfg", None, None),
        P(),
        P("req", "seq", "cfg"),
        P(None, ("req", "seq")),
        P(("req", "seq")),
        P(None, None, "req"),
        P(None, None, "req"),
        P("req", None),
        P(None, "seq"),
        P("seq", None),
        P(),
    )
    return jax.shard_map(
        on_device,
        mesh=mesh,
        in_specs=placed,
        out_specs=(P("req", "seq", "cfg"), P("req", "seq", "cfg"), P("req"), P("req")),
        check_vma=False,
    )
```

```python
import math

import jax
import jax.numpy as jnp
from jax import lax
from jax.sharding import PartitionSpec as P

D = 1536
HD = 64
PATCHC = 64
IMG = 512
STEPS = 28


SIGMA_SHIFT = 3.0
GUIDANCE = 5.0
EPSILON = 1e-06
MASKED_SCORE = -1e30


def xor_pairs(axis, distance):
    return [(source, source ^ distance) for source in range(lax.axis_size(axis))]


def shifted(fraction):
    return SIGMA_SHIFT * fraction / (1.0 + (SIGMA_SHIFT - 1.0) * fraction)


def plan(timestep):
    position = timestep.astype(jnp.float32)
    return (shifted(1.0 - position / STEPS), shifted(1.0 - (position + 1.0) / STEPS))


def time_features(sigma):
    half_width = D // 2
    frequency = jnp.exp(-math.log(10000.0) * jnp.arange(half_width, dtype=jnp.float32) / half_width)
    angles = (1000.0 * sigma)[:, None] * frequency[None, :]
    return jnp.concatenate([jnp.cos(angles), jnp.sin(angles)], axis=1)


def layer_norm(values):
    average = jnp.mean(values, axis=-1, keepdims=True)
    centred = values - average
    spread = jnp.mean(centred * centred, axis=-1, keepdims=True)
    return centred * lax.rsqrt(spread + EPSILON)


def gather_by_a2a(value, axis):
    count = lax.axis_size(axis)
    copies = jnp.broadcast_to(value[None], (count,) + value.shape)
    return lax.all_to_all(copies, axis, 0, 0, tiled=True)


def attention(queries, key_rows, value_rows, live_keys):
    scale_factor = HD ** (-0.5)
    scores = (
        jnp.einsum("qhd,khd->hqk", queries, key_rows, preferred_element_type=jnp.float32)
        * scale_factor
    )
    scores = jnp.where(live_keys[None, None, :], scores, MASKED_SCORE)
    highest = jnp.max(scores, axis=-1, keepdims=True)
    exp_scores = jnp.exp(scores - highest)
    weights = (exp_scores / jnp.sum(exp_scores, axis=-1, keepdims=True)).astype(jnp.bfloat16)
    mixture = jnp.einsum("hqk,khd->qhd", weights, value_rows, preferred_element_type=jnp.float32)
    return mixture.astype(jnp.bfloat16)


def on_device(
    img_hidden,
    txt_hidden,
    text_len,
    pooled,
    timestep,
    latent,
    mod_weight,
    mod_bias,
    img_qkv,
    txt_kv,
    out_weight,
    fc_in,
    fc_out,
    final_weight,
):
    group_size = img_hidden.shape[1]
    req_count = lax.axis_size("req")
    seq_count = lax.axis_size("seq")
    half_index = lax.axis_index("cfg")
    cond_first = half_index == 0
    split_rows = out_weight.shape[0] // 2
    own_part = lax.dynamic_slice_in_dim(out_weight, half_index * split_rows, split_rows, 0)
    gathered_part = lax.all_gather(own_part, "req", axis=0, tiled=False)
    partner_part = lax.ppermute(gathered_part, "cfg", xor_pairs("cfg", 1))
    every_weight = jnp.concatenate(
        [
            jnp.where(cond_first, gathered_part, partner_part),
            jnp.where(cond_first, partner_part, gathered_part),
        ],
        axis=1,
    )
    half_values = latent.shape[2]
    partner_latent = lax.ppermute(latent, "cfg", xor_pairs("cfg", 1))
    full_latent = jnp.concatenate(
        [
            jnp.where(cond_first, latent, partner_latent),
            jnp.where(cond_first, partner_latent, latent),
        ],
        axis=2,
    )
    current, upcoming = plan(timestep)
    activated = jax.nn.silu(pooled[0] + time_features(current)).astype(jnp.bfloat16)
    columns = jnp.dot(activated, mod_weight, preferred_element_type=jnp.float32) + mod_bias
    block_width = columns.shape[1]
    mine = lax.all_to_all(
        columns.reshape(req_count, group_size, block_width), "req", 0, 0, tiled=True
    )
    every = gather_by_a2a(mine, "seq")
    every = every.transpose(2, 1, 0, 3).reshape(group_size, req_count * seq_count * block_width)
    modulation = every.reshape(group_size, 10, 1, D)
    shift_attn, scale_attn, gate_attn = (modulation[:, 0], modulation[:, 1], modulation[:, 2])
    shift_mlp, scale_mlp, gate_mlp = (modulation[:, 3], modulation[:, 4], modulation[:, 5])
    shift_text, scale_text = (modulation[:, 6], modulation[:, 7])
    scale_final, shift_final = (modulation[:, 8], modulation[:, 9])
    img_float = img_hidden[0].astype(jnp.float32)
    img_in = (layer_norm(img_float) * (1.0 + scale_attn) + shift_attn).astype(jnp.bfloat16)
    txt_in = (
        layer_norm(txt_hidden[0].astype(jnp.float32)) * (1.0 + scale_text) + shift_text
    ).astype(jnp.bfloat16)
    row_count = img_in.shape[1]
    text_block = txt_in.shape[1]
    both = gather_by_a2a(jnp.concatenate([img_in, txt_in], axis=1), "req")
    both = both.reshape(req_count * group_size, row_count + text_block, D)
    head_width = img_qkv.shape[2]
    local_heads = head_width // HD
    qkv_columns = img_qkv.reshape(D, 3 * head_width)
    kv_columns = txt_kv.reshape(D, 2 * head_width)
    proj_img = jnp.einsum(
        "rnd,dc->rnc", both[:, :row_count], qkv_columns, preferred_element_type=jnp.float32
    ).astype(jnp.bfloat16)
    proj_txt = jnp.einsum(
        "rnd,dc->rnc", both[:, row_count:], kv_columns, preferred_element_type=jnp.float32
    ).astype(jnp.bfloat16)
    request_count = proj_img.shape[0]
    img_size = row_count * 3 * head_width
    packed = jnp.concatenate(
        [proj_img.reshape(request_count, img_size), proj_txt.reshape(request_count, -1)], axis=1
    )
    own = lax.all_to_all(packed, "seq", 0, 0, tiled=True)
    image_rows = seq_count * row_count
    text_rows = seq_count * text_block
    own_img = own[:, :img_size].reshape(image_rows, 3 * head_width)
    own_txt = own[:, img_size:].reshape(text_rows, 2 * head_width)
    queries = own_img[:, :head_width]
    key_rows = jnp.concatenate([own_img[:, head_width : 2 * head_width], own_txt[:, :head_width]], 0)
    value_rows = jnp.concatenate([own_img[:, 2 * head_width :], own_txt[:, head_width:]], 0)
    text_count = lax.dynamic_index_in_dim(text_len[0], lax.axis_index("seq"), 0, False)
    total_keys = image_rows + text_rows
    live_keys = jnp.arange(total_keys, dtype=jnp.int32) < image_rows + text_count
    attended = attention(
        queries.reshape(image_rows, local_heads, HD),
        key_rows.reshape(total_keys, local_heads, HD),
        value_rows.reshape(total_keys, local_heads, HD),
        live_keys,
    ).reshape(seq_count, row_count, head_width)
    attended_rows = lax.all_to_all(attended, "seq", 0, 0, tiled=True)
    head_columns = lax.all_to_all(
        attended_rows.reshape(req_count, group_size, row_count, head_width), "req", 0, 0, tiled=True
    )
    attn_out = jnp.einsum(
        "grnk,gkd->rnd", head_columns, every_weight, preferred_element_type=jnp.float32
    )
    img_mid = img_float + gate_attn * attn_out
    mlp_in = (layer_norm(img_mid) * (1.0 + scale_mlp) + shift_mlp).astype(jnp.bfloat16)
    all_rows = gather_by_a2a(mlp_in, "seq")
    raised = jnp.einsum("srnd,df->srnf", all_rows, fc_in, preferred_element_type=jnp.float32)
    hidden = jax.nn.gelu(raised, approximate=True).astype(jnp.bfloat16)
    mlp_terms = jnp.einsum(
        "srnf,fd->srnd", hidden, fc_out, preferred_element_type=jnp.float32
    ).astype(jnp.bfloat16)
    block_terms = lax.all_to_all(mlp_terms, "seq", 0, 0, tiled=True)
    mlp_out = jnp.sum(block_terms.astype(jnp.float32), axis=0)
    img_out = img_mid + gate_mlp * mlp_out
    final_in = (layer_norm(img_out) * (1.0 + scale_final) + shift_final).astype(jnp.bfloat16)
    own_velocity = jnp.einsum(
        "rnd,dc->rnc", final_in, final_weight, preferred_element_type=jnp.float32
    )
    other_velocity = lax.ppermute(own_velocity, "cfg", xor_pairs("cfg", 1))
    conditional = jnp.where(cond_first, own_velocity, other_velocity)
    unconditional = jnp.where(cond_first, other_velocity, own_velocity)
    guided = unconditional + GUIDANCE * (conditional - unconditional)
    offset = lax.axis_index("req") * group_size
    step_size = lax.dynamic_slice_in_dim(upcoming - current, offset, group_size, 0)
    next_latent = full_latent + step_size[:, None, None] * guided
    squares = jnp.sum(next_latent * next_latent, axis=(1, 2))
    largest = jnp.max(jnp.abs(next_latent), axis=(1, 2))
    distance = 1
    while distance < seq_count:
        stats = lax.ppermute(jnp.stack([squares, largest]), "seq", xor_pairs("seq", distance))
        squares = squares + stats[0]
        largest = jnp.maximum(largest, stats[1])
        distance *= 2
    guided = lax.dynamic_slice_in_dim(guided, half_index * half_values, half_values, 2)
    next_latent = lax.dynamic_slice_in_dim(next_latent, half_index * half_values, half_values, 2)
    latent_norm = jnp.sqrt(squares / (IMG * PATCHC))
    return (guided, next_latent, latent_norm, largest)


def solution(mesh):
    placed = (
        P("cfg", "req", "seq", None),
        P("cfg", "req", "seq", None),
        P("cfg", None),
        P("cfg", None, None),
        P(),
        P("req", "seq", "cfg"),
        P(None, ("req", "seq")),
        P(("req", "seq")),
        P(None, None, "req"),
        P(None, None, "req"),
        P("req", None),
        P(None, "seq"),
        P("seq", None),
        P(),
    )
    return jax.shard_map(
        on_device,
        mesh=mesh,
        in_specs=placed,
        out_specs=(P("req", "seq", "cfg"), P("req", "seq", "cfg"), P("req"), P("req")),
        check_vma=False,
    )
```

```python
import math

import jax
import jax.numpy as jnp
from jax import lax
from jax.sharding import PartitionSpec as P


D = 1536
HD = 64
PATCHC = 64
IMG = 512
STEPS = 28


SIGMA_SHIFT = 3.0
GUIDANCE = 5.0
EPSILON = 1e-06
MASKED_SCORE = -1e30


def xor_pairs(axis, distance):
    return [(source, source ^ distance) for source in range(lax.axis_size(axis))]


def shifted(fraction):
    return SIGMA_SHIFT * fraction / (1.0 + (SIGMA_SHIFT - 1.0) * fraction)


def plan(timestep):
    position = timestep.astype(jnp.float32)
    return (shifted(1.0 - position / STEPS), shifted(1.0 - (position + 1.0) / STEPS))


def time_features(sigma):
    half_width = D // 2
    frequency = jnp.exp(-math.log(10000.0) * jnp.arange(half_width, dtype=jnp.float32) / half_width)
    angles = (1000.0 * sigma)[:, None] * frequency[None, :]
    return jnp.concatenate([jnp.cos(angles), jnp.sin(angles)], axis=1)


def layer_norm(values):
    average = jnp.mean(values, axis=-1, keepdims=True)
    centred = values - average
    spread = jnp.mean(centred * centred, axis=-1, keepdims=True)
    return centred * lax.rsqrt(spread + EPSILON)


def gather_by_a2a(value, axis):
    count = lax.axis_size(axis)
    copies = jnp.broadcast_to(value[None], (count,) + value.shape)
    return lax.all_to_all(copies, axis, 0, 0, tiled=True)


def ring_gather(value, axis):
    count = lax.axis_size(axis)
    up = [(source, (source + 1) % count) for source in range(count)]
    down = [(source, (source - 1) % count) for source in range(count)]
    ahead = {0: value}
    from_below, from_above = value, value
    for step in range(1, count // 2 + 1):
        from_below = lax.ppermute(from_below, axis, up)
        ahead[count - step] = from_below
        if step < count - step:
            from_above = lax.ppermute(from_above, axis, down)
            ahead[step] = from_above
    return jnp.stack([ahead[k] for k in range(count)])


def attention(queries, key_rows, value_rows, live_keys):
    scale_factor = HD ** (-0.5)
    scores = (
        jnp.einsum("qhd,khd->hqk", queries, key_rows, preferred_element_type=jnp.float32)
        * scale_factor
    )
    scores = jnp.where(live_keys[None, None, :], scores, MASKED_SCORE)
    highest = jnp.max(scores, axis=-1, keepdims=True)
    exp_scores = jnp.exp(scores - highest)
    weights = (exp_scores / jnp.sum(exp_scores, axis=-1, keepdims=True)).astype(jnp.bfloat16)
    mixture = jnp.einsum("hqk,khd->qhd", weights, value_rows, preferred_element_type=jnp.float32)
    return mixture.astype(jnp.bfloat16)


def on_device(
    img_hidden,
    txt_hidden,
    text_len,
    pooled,
    timestep,
    latent,
    mod_weight,
    mod_bias,
    img_qkv,
    txt_kv,
    out_weight,
    fc_in,
    fc_out,
    final_weight,
):
    group_size = img_hidden.shape[1]
    req_count = lax.axis_size("req")
    seq_count = lax.axis_size("seq")
    half_index = lax.axis_index("cfg")
    cond_first = half_index == 0
    split_rows = out_weight.shape[0] // 2
    own_part = lax.dynamic_slice_in_dim(out_weight, half_index * split_rows, split_rows, 0)
    gathered_part = lax.all_gather(own_part, "req", axis=0, tiled=False)
    partner_part = lax.ppermute(gathered_part, "cfg", xor_pairs("cfg", 1))
    every_weight = jnp.concatenate(
        [
            jnp.where(cond_first, gathered_part, partner_part),
            jnp.where(cond_first, partner_part, gathered_part),
        ],
        axis=1,
    )
    half_values = latent.shape[2]
    partner_latent = lax.ppermute(latent, "cfg", xor_pairs("cfg", 1))
    full_latent = jnp.concatenate(
        [
            jnp.where(cond_first, latent, partner_latent),
            jnp.where(cond_first, partner_latent, latent),
        ],
        axis=2,
    )
    current, upcoming = plan(timestep)
    activated = jax.nn.silu(pooled[0] + time_features(current)).astype(jnp.bfloat16)
    columns = jnp.dot(activated, mod_weight, preferred_element_type=jnp.float32) + mod_bias
    block_width = columns.shape[1]
    mine = lax.all_to_all(
        columns.reshape(req_count, group_size, block_width), "req", 0, 0, tiled=True
    )
    every = gather_by_a2a(mine, "seq")
    every = every.transpose(2, 1, 0, 3).reshape(group_size, req_count * seq_count * block_width)
    modulation = every.reshape(group_size, 10, 1, D)
    shift_attn, scale_attn, gate_attn = (modulation[:, 0], modulation[:, 1], modulation[:, 2])
    shift_mlp, scale_mlp, gate_mlp = (modulation[:, 3], modulation[:, 4], modulation[:, 5])
    shift_text, scale_text = (modulation[:, 6], modulation[:, 7])
    scale_final, shift_final = (modulation[:, 8], modulation[:, 9])
    img_float = img_hidden[0].astype(jnp.float32)
    row_count = img_hidden.shape[2]
    text_block = txt_hidden.shape[2]
    raw_rows = ring_gather(jnp.concatenate([img_hidden[0], txt_hidden[0]], axis=1), "req")
    norm_pieces = ring_gather(
        jnp.concatenate([shift_attn, scale_attn, shift_text, scale_text], axis=1), "req"
    )
    img_in = (
        layer_norm(raw_rows[:, :, :row_count].astype(jnp.float32)) * (1.0 + norm_pieces[:, :, 1:2])
        + norm_pieces[:, :, 0:1]
    ).astype(jnp.bfloat16)
    txt_in = (
        layer_norm(raw_rows[:, :, row_count:].astype(jnp.float32)) * (1.0 + norm_pieces[:, :, 3:4])
        + norm_pieces[:, :, 2:3]
    ).astype(jnp.bfloat16)
    both = jnp.concatenate([img_in, txt_in], axis=2)
    both = both.reshape(req_count * group_size, row_count + text_block, D)
    head_width = img_qkv.shape[2]
    local_heads = head_width // HD
    qkv_columns = img_qkv.reshape(D, 3 * head_width)
    kv_columns = txt_kv.reshape(D, 2 * head_width)
    proj_img = jnp.einsum(
        "rnd,dc->rnc", both[:, :row_count], qkv_columns, preferred_element_type=jnp.float32
    ).astype(jnp.bfloat16)
    proj_txt = jnp.einsum(
        "rnd,dc->rnc", both[:, row_count:], kv_columns, preferred_element_type=jnp.float32
    ).astype(jnp.bfloat16)
    request_count = proj_img.shape[0]
    img_size = row_count * 3 * head_width
    packed = jnp.concatenate(
        [proj_img.reshape(request_count, img_size), proj_txt.reshape(request_count, -1)], axis=1
    )
    packed = jnp.roll(packed, lax.axis_index("req") * group_size, axis=0)
    own = lax.all_to_all(packed, "seq", 0, 0, tiled=True)
    image_rows = seq_count * row_count
    text_rows = seq_count * text_block
    own_img = own[:, :img_size].reshape(image_rows, 3 * head_width)
    own_txt = own[:, img_size:].reshape(text_rows, 2 * head_width)
    queries = own_img[:, :head_width]
    key_rows = jnp.concatenate([own_img[:, head_width : 2 * head_width], own_txt[:, :head_width]], 0)
    value_rows = jnp.concatenate([own_img[:, 2 * head_width :], own_txt[:, head_width:]], 0)
    text_count = lax.dynamic_index_in_dim(text_len[0], lax.axis_index("seq"), 0, False)
    total_keys = image_rows + text_rows
    live_keys = jnp.arange(total_keys, dtype=jnp.int32) < image_rows + text_count
    attended = attention(
        queries.reshape(image_rows, local_heads, HD),
        key_rows.reshape(total_keys, local_heads, HD),
        value_rows.reshape(total_keys, local_heads, HD),
        live_keys,
    ).reshape(seq_count, row_count, head_width)
    attended_rows = lax.all_to_all(attended, "seq", 0, 0, tiled=True)
    head_columns = lax.all_to_all(
        attended_rows.reshape(req_count, group_size, row_count, head_width), "req", 0, 0, tiled=True
    )
    attn_out = jnp.einsum(
        "grnk,gkd->rnd", head_columns, every_weight, preferred_element_type=jnp.float32
    )
    img_mid = img_float + gate_attn * attn_out
    mlp_in = (layer_norm(img_mid) * (1.0 + scale_mlp) + shift_mlp).astype(jnp.bfloat16)
    all_rows = gather_by_a2a(mlp_in, "seq")
    raised = jnp.einsum("srnd,df->srnf", all_rows, fc_in, preferred_element_type=jnp.float32)
    hidden = jax.nn.gelu(raised, approximate=True).astype(jnp.bfloat16)
    mlp_terms = jnp.einsum(
        "srnf,fd->srnd", hidden, fc_out, preferred_element_type=jnp.float32
    ).astype(jnp.bfloat16)
    block_terms = lax.all_to_all(mlp_terms, "seq", 0, 0, tiled=True)
    mlp_out = jnp.sum(block_terms.astype(jnp.float32), axis=0)
    img_out = img_mid + gate_mlp * mlp_out
    final_in = (layer_norm(img_out) * (1.0 + scale_final) + shift_final).astype(jnp.bfloat16)
    own_velocity = jnp.einsum(
        "rnd,dc->rnc", final_in, final_weight, preferred_element_type=jnp.float32
    )
    other_velocity = lax.ppermute(own_velocity, "cfg", xor_pairs("cfg", 1))
    conditional = jnp.where(cond_first, own_velocity, other_velocity)
    unconditional = jnp.where(cond_first, other_velocity, own_velocity)
    guided = unconditional + GUIDANCE * (conditional - unconditional)
    offset = lax.axis_index("req") * group_size
    step_size = lax.dynamic_slice_in_dim(upcoming - current, offset, group_size, 0)
    next_latent = full_latent + step_size[:, None, None] * guided
    squares = jnp.sum(next_latent * next_latent, axis=(1, 2))
    largest = jnp.max(jnp.abs(next_latent), axis=(1, 2))
    distance = 1
    while distance < seq_count:
        stats = lax.ppermute(jnp.stack([squares, largest]), "seq", xor_pairs("seq", distance))
        squares = squares + stats[0]
        largest = jnp.maximum(largest, stats[1])
        distance *= 2
    guided = lax.dynamic_slice_in_dim(guided, half_index * half_values, half_values, 2)
    next_latent = lax.dynamic_slice_in_dim(next_latent, half_index * half_values, half_values, 2)
    latent_norm = jnp.sqrt(squares / (IMG * PATCHC))
    return (guided, next_latent, latent_norm, largest)


def solution(mesh):
    placed = (
        P("cfg", "req", "seq", None),
        P("cfg", "req", "seq", None),
        P("cfg", None),
        P("cfg", None, None),
        P(),
        P("req", "seq", "cfg"),
        P(None, ("req", "seq")),
        P(("req", "seq")),
        P(None, None, "req"),
        P(None, None, "req"),
        P("req", None),
        P(None, "seq"),
        P("seq", None),
        P(),
    )
    return jax.shard_map(
        on_device,
        mesh=mesh,
        in_specs=placed,
        out_specs=(P("req", "seq", "cfg"), P("req", "seq", "cfg"), P("req"), P("req")),
        check_vma=False,
    )
```

```python
import math

import jax
import jax.numpy as jnp
from jax import lax
from jax.sharding import PartitionSpec as P


D = 1536
HD = 64
PATCHC = 64
IMG = 512
STEPS = 28


SIGMA_SHIFT = 3.0
GUIDANCE = 5.0
EPSILON = 1e-06
MASKED_SCORE = -1e30


def xor_pairs(axis, distance):
    return [(source, source ^ distance) for source in range(lax.axis_size(axis))]


def shifted(fraction):
    return SIGMA_SHIFT * fraction / (1.0 + (SIGMA_SHIFT - 1.0) * fraction)


def plan(timestep):
    position = timestep.astype(jnp.float32)
    return (shifted(1.0 - position / STEPS), shifted(1.0 - (position + 1.0) / STEPS))


def time_features(sigma):
    half_width = D // 2
    frequency = jnp.exp(-math.log(10000.0) * jnp.arange(half_width, dtype=jnp.float32) / half_width)
    angles = (1000.0 * sigma)[:, None] * frequency[None, :]
    return jnp.concatenate([jnp.cos(angles), jnp.sin(angles)], axis=1)


def layer_norm(values):
    average = jnp.mean(values, axis=-1, keepdims=True)
    centred = values - average
    spread = jnp.mean(centred * centred, axis=-1, keepdims=True)
    return centred * lax.rsqrt(spread + EPSILON)


def gather_by_a2a(value, axis):
    count = lax.axis_size(axis)
    copies = jnp.broadcast_to(value[None], (count,) + value.shape)
    return lax.all_to_all(copies, axis, 0, 0, tiled=True)


def ring_gather(value, axis):
    count = lax.axis_size(axis)
    up = [(source, (source + 1) % count) for source in range(count)]
    down = [(source, (source - 1) % count) for source in range(count)]
    ahead = {0: value}
    from_below, from_above = value, value
    for step in range(1, count // 2 + 1):
        from_below = lax.ppermute(from_below, axis, up)
        ahead[count - step] = from_below
        if step < count - step:
            from_above = lax.ppermute(from_above, axis, down)
            ahead[step] = from_above
    return jnp.stack([ahead[k] for k in range(count)])


def attention(queries, key_rows, value_rows, live_keys):
    scale_factor = HD ** (-0.5)
    scores = (
        jnp.einsum("qhd,khd->hqk", queries, key_rows, preferred_element_type=jnp.float32)
        * scale_factor
    )
    scores = jnp.where(live_keys[None, None, :], scores, MASKED_SCORE)
    highest = jnp.max(scores, axis=-1, keepdims=True)
    exp_scores = jnp.exp(scores - highest)
    weights = (exp_scores / jnp.sum(exp_scores, axis=-1, keepdims=True)).astype(jnp.bfloat16)
    mixture = jnp.einsum("hqk,khd->qhd", weights, value_rows, preferred_element_type=jnp.float32)
    return mixture.astype(jnp.bfloat16)


def on_device(
    img_hidden,
    txt_hidden,
    text_len,
    pooled,
    timestep,
    latent,
    mod_weight,
    mod_bias,
    img_qkv,
    txt_kv,
    out_weight,
    fc_in,
    fc_out,
    final_weight,
):
    group_size = img_hidden.shape[1]
    req_count = lax.axis_size("req")
    seq_count = lax.axis_size("seq")
    half_index = lax.axis_index("cfg")
    cond_first = half_index == 0
    split_rows = out_weight.shape[0] // 2
    own_part = lax.dynamic_slice_in_dim(out_weight, half_index * split_rows, split_rows, 0)
    gathered_part = lax.all_gather(own_part, "req", axis=0, tiled=False)
    partner_part = lax.ppermute(gathered_part, "cfg", xor_pairs("cfg", 1))
    every_weight = jnp.concatenate(
        [
            jnp.where(cond_first, gathered_part, partner_part),
            jnp.where(cond_first, partner_part, gathered_part),
        ],
        axis=1,
    )
    half_values = latent.shape[2]
    partner_latent = lax.ppermute(latent, "cfg", xor_pairs("cfg", 1))
    full_latent = jnp.concatenate(
        [
            jnp.where(cond_first, latent, partner_latent),
            jnp.where(cond_first, partner_latent, latent),
        ],
        axis=2,
    )
    current, upcoming = plan(timestep)
    activated = jax.nn.silu(pooled[0] + time_features(current)).astype(jnp.bfloat16)
    columns = jnp.dot(activated, mod_weight, preferred_element_type=jnp.float32) + mod_bias
    block_width = columns.shape[1]
    mine = lax.all_to_all(
        columns.reshape(req_count, group_size, block_width), "req", 0, 0, tiled=True
    )
    every = gather_by_a2a(mine, "seq")
    every = every.transpose(2, 1, 0, 3).reshape(group_size, req_count * seq_count * block_width)
    modulation = every.reshape(group_size, 10, 1, D)
    shift_attn, scale_attn, gate_attn = (modulation[:, 0], modulation[:, 1], modulation[:, 2])
    shift_mlp, scale_mlp, gate_mlp = (modulation[:, 3], modulation[:, 4], modulation[:, 5])
    shift_text, scale_text = (modulation[:, 6], modulation[:, 7])
    scale_final, shift_final = (modulation[:, 8], modulation[:, 9])
    img_float = img_hidden[0].astype(jnp.float32)
    img_in = (layer_norm(img_float) * (1.0 + scale_attn) + shift_attn).astype(jnp.bfloat16)
    txt_in = (
        layer_norm(txt_hidden[0].astype(jnp.float32)) * (1.0 + scale_text) + shift_text
    ).astype(jnp.bfloat16)
    row_count = img_in.shape[1]
    text_block = txt_in.shape[1]
    both = ring_gather(jnp.concatenate([img_in, txt_in], axis=1), "req")
    both = both.reshape(req_count * group_size, row_count + text_block, D)
    head_width = img_qkv.shape[2]
    local_heads = head_width // HD
    qkv_columns = img_qkv.reshape(D, 3 * head_width)
    kv_columns = txt_kv.reshape(D, 2 * head_width)
    proj_img = jnp.einsum(
        "rnd,dc->rnc", both[:, :row_count], qkv_columns, preferred_element_type=jnp.float32
    ).astype(jnp.bfloat16)
    proj_txt = jnp.einsum(
        "rnd,dc->rnc", both[:, row_count:], kv_columns, preferred_element_type=jnp.float32
    ).astype(jnp.bfloat16)
    request_count = proj_img.shape[0]
    img_size = row_count * 3 * head_width
    packed = jnp.concatenate(
        [proj_img.reshape(request_count, img_size), proj_txt.reshape(request_count, -1)], axis=1
    )
    packed = jnp.roll(packed, lax.axis_index("req") * group_size, axis=0)
    own = lax.all_to_all(packed, "seq", 0, 0, tiled=True)
    image_rows = seq_count * row_count
    text_rows = seq_count * text_block
    own_img = own[:, :img_size].reshape(image_rows, 3 * head_width)
    own_txt = own[:, img_size:].reshape(text_rows, 2 * head_width)
    queries = own_img[:, :head_width]
    key_rows = jnp.concatenate([own_img[:, head_width : 2 * head_width], own_txt[:, :head_width]], 0)
    value_rows = jnp.concatenate([own_img[:, 2 * head_width :], own_txt[:, head_width:]], 0)
    text_count = lax.dynamic_index_in_dim(text_len[0], lax.axis_index("seq"), 0, False)
    total_keys = image_rows + text_rows
    live_keys = jnp.arange(total_keys, dtype=jnp.int32) < image_rows + text_count
    attended = attention(
        queries.reshape(image_rows, local_heads, HD),
        key_rows.reshape(total_keys, local_heads, HD),
        value_rows.reshape(total_keys, local_heads, HD),
        live_keys,
    ).reshape(seq_count, row_count, head_width)
    attended_rows = lax.all_to_all(attended, "seq", 0, 0, tiled=True)
    head_columns = lax.all_to_all(
        attended_rows.reshape(req_count, group_size, row_count, head_width), "req", 0, 0, tiled=True
    )
    attn_out = jnp.einsum(
        "grnk,gkd->rnd", head_columns, every_weight, preferred_element_type=jnp.float32
    )
    img_mid = img_float + gate_attn * attn_out
    mlp_in = (layer_norm(img_mid) * (1.0 + scale_mlp) + shift_mlp).astype(jnp.bfloat16)
    mlp_parts = []
    for member in range(group_size):
        all_rows = gather_by_a2a(mlp_in[member], "seq")
        raised = jnp.einsum("snd,df->snf", all_rows, fc_in, preferred_element_type=jnp.float32)
        hidden = jax.nn.gelu(raised, approximate=True).astype(jnp.bfloat16)
        mlp_terms = jnp.einsum(
            "snf,fd->snd", hidden, fc_out, preferred_element_type=jnp.float32
        ).astype(jnp.bfloat16)
        block_terms = lax.all_to_all(mlp_terms, "seq", 0, 0, tiled=True)
        mlp_parts.append(jnp.sum(block_terms.astype(jnp.float32), axis=0))
    mlp_out = jnp.stack(mlp_parts)
    img_out = img_mid + gate_mlp * mlp_out
    final_in = (layer_norm(img_out) * (1.0 + scale_final) + shift_final).astype(jnp.bfloat16)
    own_velocity = jnp.einsum(
        "rnd,dc->rnc", final_in, final_weight, preferred_element_type=jnp.float32
    )
    other_velocity = lax.ppermute(own_velocity, "cfg", xor_pairs("cfg", 1))
    conditional = jnp.where(cond_first, own_velocity, other_velocity)
    unconditional = jnp.where(cond_first, other_velocity, own_velocity)
    guided = unconditional + GUIDANCE * (conditional - unconditional)
    offset = lax.axis_index("req") * group_size
    step_size = lax.dynamic_slice_in_dim(upcoming - current, offset, group_size, 0)
    next_latent = full_latent + step_size[:, None, None] * guided
    squares = jnp.sum(next_latent * next_latent, axis=(1, 2))
    largest = jnp.max(jnp.abs(next_latent), axis=(1, 2))
    distance = 1
    while distance < seq_count:
        stats = lax.ppermute(jnp.stack([squares, largest]), "seq", xor_pairs("seq", distance))
        squares = squares + stats[0]
        largest = jnp.maximum(largest, stats[1])
        distance *= 2
    guided = lax.dynamic_slice_in_dim(guided, half_index * half_values, half_values, 2)
    next_latent = lax.dynamic_slice_in_dim(next_latent, half_index * half_values, half_values, 2)
    latent_norm = jnp.sqrt(squares / (IMG * PATCHC))
    return (guided, next_latent, latent_norm, largest)


def solution(mesh):
    placed = (
        P("cfg", "req", "seq", None),
        P("cfg", "req", "seq", None),
        P("cfg", None),
        P("cfg", None, None),
        P(),
        P("req", "seq", "cfg"),
        P(None, ("req", "seq")),
        P(("req", "seq")),
        P(None, None, "req"),
        P(None, None, "req"),
        P("req", None),
        P(None, "seq"),
        P("seq", None),
        P(),
    )
    return jax.shard_map(
        on_device,
        mesh=mesh,
        in_specs=placed,
        out_specs=(P("req", "seq", "cfg"), P("req", "seq", "cfg"), P("req"), P("req")),
        check_vma=False,
    )
```

```python
import math

import jax
import jax.numpy as jnp
from jax import lax
from jax.sharding import PartitionSpec as P


D = 1536
HD = 64
PATCHC = 64
IMG = 512
STEPS = 28


SIGMA_SHIFT = 3.0
GUIDANCE = 5.0
EPSILON = 1e-06
MASKED_SCORE = -1e30


def xor_pairs(axis, distance):
    return [(source, source ^ distance) for source in range(lax.axis_size(axis))]


def shifted(fraction):
    return SIGMA_SHIFT * fraction / (1.0 + (SIGMA_SHIFT - 1.0) * fraction)


def plan(timestep):
    position = timestep.astype(jnp.float32)
    return (shifted(1.0 - position / STEPS), shifted(1.0 - (position + 1.0) / STEPS))


def time_features(sigma):
    half_width = D // 2
    frequency = jnp.exp(-math.log(10000.0) * jnp.arange(half_width, dtype=jnp.float32) / half_width)
    angles = (1000.0 * sigma)[:, None] * frequency[None, :]
    return jnp.concatenate([jnp.cos(angles), jnp.sin(angles)], axis=1)


def layer_norm(values):
    average = jnp.mean(values, axis=-1, keepdims=True)
    centred = values - average
    spread = jnp.mean(centred * centred, axis=-1, keepdims=True)
    return centred * lax.rsqrt(spread + EPSILON)


def gather_by_a2a(value, axis):
    count = lax.axis_size(axis)
    copies = jnp.broadcast_to(value[None], (count,) + value.shape)
    return lax.all_to_all(copies, axis, 0, 0, tiled=True)


def ring_gather(value, axis):
    count = lax.axis_size(axis)
    up = [(source, (source + 1) % count) for source in range(count)]
    down = [(source, (source - 1) % count) for source in range(count)]
    ahead = {0: value}
    from_below, from_above = value, value
    for step in range(1, count // 2 + 1):
        from_below = lax.ppermute(from_below, axis, up)
        ahead[count - step] = from_below
        if step < count - step:
            from_above = lax.ppermute(from_above, axis, down)
            ahead[step] = from_above
    return jnp.stack([ahead[k] for k in range(count)])


def attention(queries, key_rows, value_rows, live_keys):
    scale_factor = HD ** (-0.5)
    scores = (
        jnp.einsum("qhd,khd->hqk", queries, key_rows, preferred_element_type=jnp.float32)
        * scale_factor
    )
    scores = jnp.where(live_keys[None, None, :], scores, MASKED_SCORE)
    highest = jnp.max(scores, axis=-1, keepdims=True)
    exp_scores = jnp.exp(scores - highest)
    weights = (exp_scores / jnp.sum(exp_scores, axis=-1, keepdims=True)).astype(jnp.bfloat16)
    mixture = jnp.einsum("hqk,khd->qhd", weights, value_rows, preferred_element_type=jnp.float32)
    return mixture.astype(jnp.bfloat16)


def on_device(
    img_hidden,
    txt_hidden,
    text_len,
    pooled,
    timestep,
    latent,
    mod_weight,
    mod_bias,
    img_qkv,
    txt_kv,
    out_weight,
    fc_in,
    fc_out,
    final_weight,
):
    group_size = img_hidden.shape[1]
    req_count = lax.axis_size("req")
    seq_count = lax.axis_size("seq")
    half_index = lax.axis_index("cfg")
    cond_first = half_index == 0
    split_rows = out_weight.shape[0] // 2
    own_part = lax.dynamic_slice_in_dim(out_weight, half_index * split_rows, split_rows, 0)
    gathered_part = ring_gather(own_part, "req")
    partner_part = lax.ppermute(gathered_part, "cfg", xor_pairs("cfg", 1))
    every_weight = jnp.concatenate(
        [
            jnp.where(cond_first, gathered_part, partner_part),
            jnp.where(cond_first, partner_part, gathered_part),
        ],
        axis=1,
    )
    half_values = latent.shape[2]
    partner_latent = lax.ppermute(latent, "cfg", xor_pairs("cfg", 1))
    full_latent = jnp.concatenate(
        [
            jnp.where(cond_first, latent, partner_latent),
            jnp.where(cond_first, partner_latent, latent),
        ],
        axis=2,
    )
    current, upcoming = plan(timestep)
    activated = jax.nn.silu(pooled[0] + time_features(current)).astype(jnp.bfloat16)
    columns = jnp.dot(activated, mod_weight, preferred_element_type=jnp.float32) + mod_bias
    block_width = columns.shape[1]
    mine = lax.all_to_all(
        columns.reshape(req_count, group_size, block_width), "req", 0, 0, tiled=True
    )
    every = gather_by_a2a(mine, "seq")
    every = every.transpose(2, 1, 0, 3).reshape(group_size, req_count * seq_count * block_width)
    modulation = every.reshape(group_size, 10, 1, D)
    shift_attn, scale_attn, gate_attn = (modulation[:, 0], modulation[:, 1], modulation[:, 2])
    shift_mlp, scale_mlp, gate_mlp = (modulation[:, 3], modulation[:, 4], modulation[:, 5])
    shift_text, scale_text = (modulation[:, 6], modulation[:, 7])
    scale_final, shift_final = (modulation[:, 8], modulation[:, 9])
    img_float = img_hidden[0].astype(jnp.float32)
    img_in = (layer_norm(img_float) * (1.0 + scale_attn) + shift_attn).astype(jnp.bfloat16)
    txt_in = (
        layer_norm(txt_hidden[0].astype(jnp.float32)) * (1.0 + scale_text) + shift_text
    ).astype(jnp.bfloat16)
    row_count = img_in.shape[1]
    text_block = txt_in.shape[1]
    both = ring_gather(jnp.concatenate([img_in, txt_in], axis=1), "req")
    both = both.reshape(req_count * group_size, row_count + text_block, D)
    head_width = img_qkv.shape[2]
    local_heads = head_width // HD
    qkv_columns = img_qkv.reshape(D, 3 * head_width)
    kv_columns = txt_kv.reshape(D, 2 * head_width)
    proj_img = jnp.einsum(
        "rnd,dc->rnc", both[:, :row_count], qkv_columns, preferred_element_type=jnp.float32
    ).astype(jnp.bfloat16)
    proj_txt = jnp.einsum(
        "rnd,dc->rnc", both[:, row_count:], kv_columns, preferred_element_type=jnp.float32
    ).astype(jnp.bfloat16)
    request_count = proj_img.shape[0]
    img_size = row_count * 3 * head_width
    packed = jnp.concatenate(
        [proj_img.reshape(request_count, img_size), proj_txt.reshape(request_count, -1)], axis=1
    )
    packed = jnp.roll(packed, lax.axis_index("req") * group_size, axis=0)
    own = lax.all_to_all(packed, "seq", 0, 0, tiled=True)
    image_rows = seq_count * row_count
    text_rows = seq_count * text_block
    own_img = own[:, :img_size].reshape(image_rows, 3 * head_width)
    own_txt = own[:, img_size:].reshape(text_rows, 2 * head_width)
    queries = own_img[:, :head_width]
    key_rows = jnp.concatenate([own_img[:, head_width : 2 * head_width], own_txt[:, :head_width]], 0)
    value_rows = jnp.concatenate([own_img[:, 2 * head_width :], own_txt[:, head_width:]], 0)
    text_count = lax.dynamic_index_in_dim(text_len[0], lax.axis_index("seq"), 0, False)
    total_keys = image_rows + text_rows
    live_keys = jnp.arange(total_keys, dtype=jnp.int32) < image_rows + text_count
    attended = attention(
        queries.reshape(image_rows, local_heads, HD),
        key_rows.reshape(total_keys, local_heads, HD),
        value_rows.reshape(total_keys, local_heads, HD),
        live_keys,
    ).reshape(seq_count, row_count, head_width)
    attended_rows = lax.all_to_all(attended, "seq", 0, 0, tiled=True)
    head_columns = lax.all_to_all(
        attended_rows.reshape(req_count, group_size, row_count, head_width), "req", 0, 0, tiled=True
    )
    head_columns = jnp.roll(head_columns, -lax.axis_index("req"), axis=0)
    attn_out = jnp.einsum(
        "grnk,gkd->rnd", head_columns, every_weight, preferred_element_type=jnp.float32
    )
    img_mid = img_float + gate_attn * attn_out
    mlp_in = (layer_norm(img_mid) * (1.0 + scale_mlp) + shift_mlp).astype(jnp.bfloat16)
    all_rows = gather_by_a2a(mlp_in, "seq")
    raised = jnp.einsum("srnd,df->srnf", all_rows, fc_in, preferred_element_type=jnp.float32)
    hidden = jax.nn.gelu(raised, approximate=True).astype(jnp.bfloat16)
    mlp_terms = jnp.einsum(
        "srnf,fd->srnd", hidden, fc_out, preferred_element_type=jnp.float32
    ).astype(jnp.bfloat16)
    block_terms = lax.all_to_all(mlp_terms, "seq", 0, 0, tiled=True)
    mlp_out = jnp.sum(block_terms.astype(jnp.float32), axis=0)
    img_out = img_mid + gate_mlp * mlp_out
    final_in = (layer_norm(img_out) * (1.0 + scale_final) + shift_final).astype(jnp.bfloat16)
    own_velocity = jnp.einsum(
        "rnd,dc->rnc", final_in, final_weight, preferred_element_type=jnp.float32
    )
    other_velocity = lax.ppermute(own_velocity, "cfg", xor_pairs("cfg", 1))
    conditional = jnp.where(cond_first, own_velocity, other_velocity)
    unconditional = jnp.where(cond_first, other_velocity, own_velocity)
    guided = unconditional + GUIDANCE * (conditional - unconditional)
    offset = lax.axis_index("req") * group_size
    step_size = lax.dynamic_slice_in_dim(upcoming - current, offset, group_size, 0)
    next_latent = full_latent + step_size[:, None, None] * guided
    squares = jnp.sum(next_latent * next_latent, axis=(1, 2))
    largest = jnp.max(jnp.abs(next_latent), axis=(1, 2))
    distance = 1
    while distance < seq_count:
        stats = lax.ppermute(jnp.stack([squares, largest]), "seq", xor_pairs("seq", distance))
        squares = squares + stats[0]
        largest = jnp.maximum(largest, stats[1])
        distance *= 2
    guided = lax.dynamic_slice_in_dim(guided, half_index * half_values, half_values, 2)
    next_latent = lax.dynamic_slice_in_dim(next_latent, half_index * half_values, half_values, 2)
    latent_norm = jnp.sqrt(squares / (IMG * PATCHC))
    return (guided, next_latent, latent_norm, largest)


def solution(mesh):
    placed = (
        P("cfg", "req", "seq", None),
        P("cfg", "req", "seq", None),
        P("cfg", None),
        P("cfg", None, None),
        P(),
        P("req", "seq", "cfg"),
        P(None, ("req", "seq")),
        P(("req", "seq")),
        P(None, None, "req"),
        P(None, None, "req"),
        P("req", None),
        P(None, "seq"),
        P("seq", None),
        P(),
    )
    return jax.shard_map(
        on_device,
        mesh=mesh,
        in_specs=placed,
        out_specs=(P("req", "seq", "cfg"), P("req", "seq", "cfg"), P("req"), P("req")),
        check_vma=False,
    )
```

```python
import math

import jax
import jax.numpy as jnp
from jax import lax
from jax.sharding import PartitionSpec as P


D = 1536
HD = 64
PATCHC = 64
IMG = 512
STEPS = 28


SIGMA_SHIFT = 3.0
GUIDANCE = 5.0
EPSILON = 1e-06
MASKED_SCORE = -1e30


def xor_pairs(axis, distance):
    return [(source, source ^ distance) for source in range(lax.axis_size(axis))]


def shifted(fraction):
    return SIGMA_SHIFT * fraction / (1.0 + (SIGMA_SHIFT - 1.0) * fraction)


def plan(timestep):
    position = timestep.astype(jnp.float32)
    return (shifted(1.0 - position / STEPS), shifted(1.0 - (position + 1.0) / STEPS))


def time_features(sigma):
    half_width = D // 2
    frequency = jnp.exp(-math.log(10000.0) * jnp.arange(half_width, dtype=jnp.float32) / half_width)
    angles = (1000.0 * sigma)[:, None] * frequency[None, :]
    return jnp.concatenate([jnp.cos(angles), jnp.sin(angles)], axis=1)


def layer_norm(values):
    average = jnp.mean(values, axis=-1, keepdims=True)
    centred = values - average
    spread = jnp.mean(centred * centred, axis=-1, keepdims=True)
    return centred * lax.rsqrt(spread + EPSILON)


def gather_by_a2a(value, axis):
    count = lax.axis_size(axis)
    copies = jnp.broadcast_to(value[None], (count,) + value.shape)
    return lax.all_to_all(copies, axis, 0, 0, tiled=True)


def ring_gather(value, axis, after=None):
    count = lax.axis_size(axis)
    up = [(source, (source + 1) % count) for source in range(count)]
    down = [(source, (source - 1) % count) for source in range(count)]
    ahead = {0: value}
    from_below, from_above = value, value
    for step in range(1, count // 2 + 1):
        if step == 2 and after is not None:
            from_below, from_above, _ = lax.optimization_barrier((from_below, from_above, after))
        from_below = lax.ppermute(from_below, axis, up)
        ahead[count - step] = from_below
        if step < count - step:
            from_above = lax.ppermute(from_above, axis, down)
            ahead[step] = from_above
    return jnp.stack([ahead[k] for k in range(count)])


def attention(queries, key_rows, value_rows, live_keys):
    scale_factor = HD ** (-0.5)
    scores = (
        jnp.einsum("qhd,khd->hqk", queries, key_rows, preferred_element_type=jnp.float32)
        * scale_factor
    )
    scores = jnp.where(live_keys[None, None, :], scores, MASKED_SCORE)
    highest = jnp.max(scores, axis=-1, keepdims=True)
    exp_scores = jnp.exp(scores - highest)
    weights = (exp_scores / jnp.sum(exp_scores, axis=-1, keepdims=True)).astype(jnp.bfloat16)
    mixture = jnp.einsum("hqk,khd->qhd", weights, value_rows, preferred_element_type=jnp.float32)
    return mixture.astype(jnp.bfloat16)


def on_device(
    img_hidden,
    txt_hidden,
    text_len,
    pooled,
    timestep,
    latent,
    mod_weight,
    mod_bias,
    img_qkv,
    txt_kv,
    out_weight,
    fc_in,
    fc_out,
    final_weight,
):
    group_size = img_hidden.shape[1]
    req_count = lax.axis_size("req")
    seq_count = lax.axis_size("seq")
    half_index = lax.axis_index("cfg")
    cond_first = half_index == 0
    half_values = latent.shape[2]
    partner_latent = lax.ppermute(latent, "cfg", xor_pairs("cfg", 1))
    full_latent = jnp.concatenate(
        [
            jnp.where(cond_first, latent, partner_latent),
            jnp.where(cond_first, partner_latent, latent),
        ],
        axis=2,
    )
    current, upcoming = plan(timestep)
    activated = jax.nn.silu(pooled[0] + time_features(current)).astype(jnp.bfloat16)
    columns = jnp.dot(activated, mod_weight, preferred_element_type=jnp.float32) + mod_bias
    block_width = columns.shape[1]
    mine = lax.all_to_all(
        columns.reshape(req_count, group_size, block_width), "req", 0, 0, tiled=True
    )
    every = gather_by_a2a(mine, "seq")
    every = every.transpose(2, 1, 0, 3).reshape(group_size, req_count * seq_count * block_width)
    modulation = every.reshape(group_size, 10, 1, D)
    shift_attn, scale_attn, gate_attn = (modulation[:, 0], modulation[:, 1], modulation[:, 2])
    shift_mlp, scale_mlp, gate_mlp = (modulation[:, 3], modulation[:, 4], modulation[:, 5])
    shift_text, scale_text = (modulation[:, 6], modulation[:, 7])
    scale_final, shift_final = (modulation[:, 8], modulation[:, 9])
    img_float = img_hidden[0].astype(jnp.float32)
    img_in = (layer_norm(img_float) * (1.0 + scale_attn) + shift_attn).astype(jnp.bfloat16)
    txt_in = (
        layer_norm(txt_hidden[0].astype(jnp.float32)) * (1.0 + scale_text) + shift_text
    ).astype(jnp.bfloat16)
    row_count = img_in.shape[1]
    text_block = txt_in.shape[1]
    both = ring_gather(jnp.concatenate([img_in, txt_in], axis=1), "req")
    both = both.reshape(req_count * group_size, row_count + text_block, D)
    split_rows = out_weight.shape[0] // 2
    own_part = lax.dynamic_slice_in_dim(out_weight, half_index * split_rows, split_rows, 0)
    gathered_part = ring_gather(own_part, "req", after=both)
    partner_part = lax.ppermute(gathered_part, "cfg", xor_pairs("cfg", 1))
    every_weight = jnp.concatenate(
        [
            jnp.where(cond_first, gathered_part, partner_part),
            jnp.where(cond_first, partner_part, gathered_part),
        ],
        axis=1,
    )
    head_width = img_qkv.shape[2]
    local_heads = head_width // HD
    qkv_columns = img_qkv.reshape(D, 3 * head_width)
    kv_columns = txt_kv.reshape(D, 2 * head_width)
    proj_img = jnp.einsum(
        "rnd,dc->rnc", both[:, :row_count], qkv_columns, preferred_element_type=jnp.float32
    ).astype(jnp.bfloat16)
    proj_txt = jnp.einsum(
        "rnd,dc->rnc", both[:, row_count:], kv_columns, preferred_element_type=jnp.float32
    ).astype(jnp.bfloat16)
    request_count = proj_img.shape[0]
    img_size = row_count * 3 * head_width
    packed = jnp.concatenate(
        [proj_img.reshape(request_count, img_size), proj_txt.reshape(request_count, -1)], axis=1
    )
    packed = jnp.roll(packed, lax.axis_index("req") * group_size, axis=0)
    own = lax.all_to_all(packed, "seq", 0, 0, tiled=True)
    image_rows = seq_count * row_count
    text_rows = seq_count * text_block
    own_img = own[:, :img_size].reshape(image_rows, 3 * head_width)
    own_txt = own[:, img_size:].reshape(text_rows, 2 * head_width)
    queries = own_img[:, :head_width]
    key_rows = jnp.concatenate([own_img[:, head_width : 2 * head_width], own_txt[:, :head_width]], 0)
    value_rows = jnp.concatenate([own_img[:, 2 * head_width :], own_txt[:, head_width:]], 0)
    text_count = lax.dynamic_index_in_dim(text_len[0], lax.axis_index("seq"), 0, False)
    total_keys = image_rows + text_rows
    live_keys = jnp.arange(total_keys, dtype=jnp.int32) < image_rows + text_count
    attended = attention(
        queries.reshape(image_rows, local_heads, HD),
        key_rows.reshape(total_keys, local_heads, HD),
        value_rows.reshape(total_keys, local_heads, HD),
        live_keys,
    ).reshape(seq_count, row_count, head_width)
    attended_rows = lax.all_to_all(attended, "seq", 0, 0, tiled=True)
    head_columns = lax.all_to_all(
        attended_rows.reshape(req_count, group_size, row_count, head_width), "req", 0, 0, tiled=True
    )
    head_columns = jnp.roll(head_columns, -lax.axis_index("req"), axis=0)
    attn_out = jnp.einsum(
        "grnk,gkd->rnd", head_columns, every_weight, preferred_element_type=jnp.float32
    )
    img_mid = img_float + gate_attn * attn_out
    mlp_in = (layer_norm(img_mid) * (1.0 + scale_mlp) + shift_mlp).astype(jnp.bfloat16)
    all_rows = gather_by_a2a(mlp_in, "seq")
    raised = jnp.einsum("srnd,df->srnf", all_rows, fc_in, preferred_element_type=jnp.float32)
    hidden = jax.nn.gelu(raised, approximate=True).astype(jnp.bfloat16)
    mlp_terms = jnp.einsum(
        "srnf,fd->srnd", hidden, fc_out, preferred_element_type=jnp.float32
    ).astype(jnp.bfloat16)
    block_terms = lax.all_to_all(mlp_terms, "seq", 0, 0, tiled=True)
    mlp_out = jnp.sum(block_terms.astype(jnp.float32), axis=0)
    img_out = img_mid + gate_mlp * mlp_out
    final_in = (layer_norm(img_out) * (1.0 + scale_final) + shift_final).astype(jnp.bfloat16)
    own_velocity = jnp.einsum(
        "rnd,dc->rnc", final_in, final_weight, preferred_element_type=jnp.float32
    )
    other_velocity = lax.ppermute(own_velocity, "cfg", xor_pairs("cfg", 1))
    conditional = jnp.where(cond_first, own_velocity, other_velocity)
    unconditional = jnp.where(cond_first, other_velocity, own_velocity)
    guided = unconditional + GUIDANCE * (conditional - unconditional)
    offset = lax.axis_index("req") * group_size
    step_size = lax.dynamic_slice_in_dim(upcoming - current, offset, group_size, 0)
    next_latent = full_latent + step_size[:, None, None] * guided
    squares = jnp.sum(next_latent * next_latent, axis=(1, 2))
    largest = jnp.max(jnp.abs(next_latent), axis=(1, 2))
    distance = 1
    while distance < seq_count:
        stats = lax.ppermute(jnp.stack([squares, largest]), "seq", xor_pairs("seq", distance))
        squares = squares + stats[0]
        largest = jnp.maximum(largest, stats[1])
        distance *= 2
    guided = lax.dynamic_slice_in_dim(guided, half_index * half_values, half_values, 2)
    next_latent = lax.dynamic_slice_in_dim(next_latent, half_index * half_values, half_values, 2)
    latent_norm = jnp.sqrt(squares / (IMG * PATCHC))
    return (guided, next_latent, latent_norm, largest)


def solution(mesh):
    placed = (
        P("cfg", "req", "seq", None),
        P("cfg", "req", "seq", None),
        P("cfg", None),
        P("cfg", None, None),
        P(),
        P("req", "seq", "cfg"),
        P(None, ("req", "seq")),
        P(("req", "seq")),
        P(None, None, "req"),
        P(None, None, "req"),
        P("req", None),
        P(None, "seq"),
        P("seq", None),
        P(),
    )
    return jax.shard_map(
        on_device,
        mesh=mesh,
        in_specs=placed,
        out_specs=(P("req", "seq", "cfg"), P("req", "seq", "cfg"), P("req"), P("req")),
        check_vma=False,
    )
```

```python
import math

import jax
import jax.numpy as jnp
from jax import lax
from jax.sharding import PartitionSpec as P


D = 1536
HD = 64
PATCHC = 64
IMG = 512
STEPS = 28


SIGMA_SHIFT = 3.0
GUIDANCE = 5.0
EPSILON = 1e-06
MASKED_SCORE = -1e30


def xor_pairs(axis, distance):
    return [(source, source ^ distance) for source in range(lax.axis_size(axis))]


def shifted(fraction):
    return SIGMA_SHIFT * fraction / (1.0 + (SIGMA_SHIFT - 1.0) * fraction)


def plan(timestep):
    position = timestep.astype(jnp.float32)
    return (shifted(1.0 - position / STEPS), shifted(1.0 - (position + 1.0) / STEPS))


def time_features(sigma):
    half_width = D // 2
    frequency = jnp.exp(-math.log(10000.0) * jnp.arange(half_width, dtype=jnp.float32) / half_width)
    angles = (1000.0 * sigma)[:, None] * frequency[None, :]
    return jnp.concatenate([jnp.cos(angles), jnp.sin(angles)], axis=1)


def layer_norm(values):
    average = jnp.mean(values, axis=-1, keepdims=True)
    centred = values - average
    spread = jnp.mean(centred * centred, axis=-1, keepdims=True)
    return centred * lax.rsqrt(spread + EPSILON)


def gather_by_a2a(value, axis):
    count = lax.axis_size(axis)
    copies = jnp.broadcast_to(value[None], (count,) + value.shape)
    return lax.all_to_all(copies, axis, 0, 0, tiled=True)


def ring_gather(value, axis):
    count = lax.axis_size(axis)
    up = [(source, (source + 1) % count) for source in range(count)]
    down = [(source, (source - 1) % count) for source in range(count)]
    ahead = {0: value}
    from_below, from_above = value, value
    for step in range(1, count // 2 + 1):
        from_below = lax.ppermute(from_below, axis, up)
        ahead[count - step] = from_below
        if step < count - step:
            from_above = lax.ppermute(from_above, axis, down)
            ahead[step] = from_above
    return jnp.stack([ahead[k] for k in range(count)])


def attention(queries, key_rows, value_rows, live_keys):
    scale_factor = HD ** (-0.5)
    scores = (
        jnp.einsum("qhd,khd->hqk", queries, key_rows, preferred_element_type=jnp.float32)
        * scale_factor
    )
    scores = jnp.where(live_keys[None, None, :], scores, MASKED_SCORE)
    highest = jnp.max(scores, axis=-1, keepdims=True)
    exp_scores = jnp.exp(scores - highest)
    weights = (exp_scores / jnp.sum(exp_scores, axis=-1, keepdims=True)).astype(jnp.bfloat16)
    mixture = jnp.einsum("hqk,khd->qhd", weights, value_rows, preferred_element_type=jnp.float32)
    return mixture.astype(jnp.bfloat16)


def on_device(
    img_hidden,
    txt_hidden,
    text_len,
    pooled,
    timestep,
    latent,
    mod_weight,
    mod_bias,
    img_qkv,
    txt_kv,
    out_weight,
    fc_in,
    fc_out,
    final_weight,
):
    group_size = img_hidden.shape[1]
    req_count = lax.axis_size("req")
    seq_count = lax.axis_size("seq")
    half_index = lax.axis_index("cfg")
    cond_first = half_index == 0
    split_rows = out_weight.shape[0] // 2
    own_part = lax.dynamic_slice_in_dim(out_weight, half_index * split_rows, split_rows, 0)
    gathered_part = ring_gather(own_part, "req")
    partner_part = lax.ppermute(gathered_part, "cfg", xor_pairs("cfg", 1))
    every_weight = jnp.concatenate(
        [
            jnp.where(cond_first, gathered_part, partner_part),
            jnp.where(cond_first, partner_part, gathered_part),
        ],
        axis=1,
    )
    half_values = latent.shape[2]
    partner_latent = lax.ppermute(latent, "cfg", xor_pairs("cfg", 1))
    full_latent = jnp.concatenate(
        [
            jnp.where(cond_first, latent, partner_latent),
            jnp.where(cond_first, partner_latent, latent),
        ],
        axis=2,
    )
    current, upcoming = plan(timestep)
    activated = jax.nn.silu(pooled[0] + time_features(current)).astype(jnp.bfloat16)
    columns = jnp.dot(activated, mod_weight, preferred_element_type=jnp.float32) + mod_bias
    block_width = columns.shape[1]
    copies = jnp.broadcast_to(
        columns.reshape(req_count, 1, group_size, block_width),
        (req_count, seq_count, group_size, block_width),
    ).reshape(req_count * seq_count, group_size, block_width)
    every = lax.all_to_all(copies, ("req", "seq"), 0, 0, tiled=True)
    every = every.transpose(1, 0, 2).reshape(group_size, req_count * seq_count * block_width)
    modulation = every.reshape(group_size, 10, 1, D)
    shift_attn, scale_attn, gate_attn = (modulation[:, 0], modulation[:, 1], modulation[:, 2])
    shift_mlp, scale_mlp, gate_mlp = (modulation[:, 3], modulation[:, 4], modulation[:, 5])
    shift_text, scale_text = (modulation[:, 6], modulation[:, 7])
    scale_final, shift_final = (modulation[:, 8], modulation[:, 9])
    img_float = img_hidden[0].astype(jnp.float32)
    img_in = (layer_norm(img_float) * (1.0 + scale_attn) + shift_attn).astype(jnp.bfloat16)
    txt_in = (
        layer_norm(txt_hidden[0].astype(jnp.float32)) * (1.0 + scale_text) + shift_text
    ).astype(jnp.bfloat16)
    row_count = img_in.shape[1]
    text_block = txt_in.shape[1]
    both = ring_gather(jnp.concatenate([img_in, txt_in], axis=1), "req")
    both = both.reshape(req_count * group_size, row_count + text_block, D)
    head_width = img_qkv.shape[2]
    local_heads = head_width // HD
    qkv_columns = img_qkv.reshape(D, 3 * head_width)
    kv_columns = txt_kv.reshape(D, 2 * head_width)
    proj_img = jnp.einsum(
        "rnd,dc->rnc", both[:, :row_count], qkv_columns, preferred_element_type=jnp.float32
    ).astype(jnp.bfloat16)
    proj_txt = jnp.einsum(
        "rnd,dc->rnc", both[:, row_count:], kv_columns, preferred_element_type=jnp.float32
    ).astype(jnp.bfloat16)
    request_count = proj_img.shape[0]
    img_size = row_count * 3 * head_width
    packed = jnp.concatenate(
        [proj_img.reshape(request_count, img_size), proj_txt.reshape(request_count, -1)], axis=1
    )
    packed = jnp.roll(packed, lax.axis_index("req") * group_size, axis=0)
    own = lax.all_to_all(packed, "seq", 0, 0, tiled=True)
    image_rows = seq_count * row_count
    text_rows = seq_count * text_block
    own_img = own[:, :img_size].reshape(image_rows, 3 * head_width)
    own_txt = own[:, img_size:].reshape(text_rows, 2 * head_width)
    queries = own_img[:, :head_width]
    key_rows = jnp.concatenate([own_img[:, head_width : 2 * head_width], own_txt[:, :head_width]], 0)
    value_rows = jnp.concatenate([own_img[:, 2 * head_width :], own_txt[:, head_width:]], 0)
    text_count = lax.dynamic_index_in_dim(text_len[0], lax.axis_index("seq"), 0, False)
    total_keys = image_rows + text_rows
    live_keys = jnp.arange(total_keys, dtype=jnp.int32) < image_rows + text_count
    attended = attention(
        queries.reshape(image_rows, local_heads, HD),
        key_rows.reshape(total_keys, local_heads, HD),
        value_rows.reshape(total_keys, local_heads, HD),
        live_keys,
    ).reshape(seq_count, row_count, head_width)
    attended_rows = lax.all_to_all(attended, "seq", 0, 0, tiled=True)
    head_columns = lax.all_to_all(
        attended_rows.reshape(req_count, group_size, row_count, head_width), "req", 0, 0, tiled=True
    )
    head_columns = jnp.roll(head_columns, -lax.axis_index("req"), axis=0)
    attn_out = jnp.einsum(
        "grnk,gkd->rnd", head_columns, every_weight, preferred_element_type=jnp.float32
    )
    img_mid = img_float + gate_attn * attn_out
    mlp_in = (layer_norm(img_mid) * (1.0 + scale_mlp) + shift_mlp).astype(jnp.bfloat16)
    all_rows = gather_by_a2a(mlp_in, "seq")
    raised = jnp.einsum("srnd,df->srnf", all_rows, fc_in, preferred_element_type=jnp.float32)
    hidden = jax.nn.gelu(raised, approximate=True).astype(jnp.bfloat16)
    mlp_terms = jnp.einsum(
        "srnf,fd->srnd", hidden, fc_out, preferred_element_type=jnp.float32
    ).astype(jnp.bfloat16)
    block_terms = lax.all_to_all(mlp_terms, "seq", 0, 0, tiled=True)
    mlp_out = jnp.sum(block_terms.astype(jnp.float32), axis=0)
    img_out = img_mid + gate_mlp * mlp_out
    final_in = (layer_norm(img_out) * (1.0 + scale_final) + shift_final).astype(jnp.bfloat16)
    own_velocity = jnp.einsum(
        "rnd,dc->rnc", final_in, final_weight, preferred_element_type=jnp.float32
    )
    other_velocity = lax.ppermute(own_velocity, "cfg", xor_pairs("cfg", 1))
    conditional = jnp.where(cond_first, own_velocity, other_velocity)
    unconditional = jnp.where(cond_first, other_velocity, own_velocity)
    guided = unconditional + GUIDANCE * (conditional - unconditional)
    offset = lax.axis_index("req") * group_size
    step_size = lax.dynamic_slice_in_dim(upcoming - current, offset, group_size, 0)
    next_latent = full_latent + step_size[:, None, None] * guided
    squares = jnp.sum(next_latent * next_latent, axis=(1, 2))
    largest = jnp.max(jnp.abs(next_latent), axis=(1, 2))
    stats = gather_by_a2a(jnp.stack([squares, largest]), "seq")
    squares = jnp.sum(stats[:, 0], axis=0)
    largest = jnp.max(stats[:, 1], axis=0)
    guided = lax.dynamic_slice_in_dim(guided, half_index * half_values, half_values, 2)
    next_latent = lax.dynamic_slice_in_dim(next_latent, half_index * half_values, half_values, 2)
    latent_norm = jnp.sqrt(squares / (IMG * PATCHC))
    return (guided, next_latent, latent_norm, largest)


def solution(mesh):
    placed = (
        P("cfg", "req", "seq", None),
        P("cfg", "req", "seq", None),
        P("cfg", None),
        P("cfg", None, None),
        P(),
        P("req", "seq", "cfg"),
        P(None, ("req", "seq")),
        P(("req", "seq")),
        P(None, None, "req"),
        P(None, None, "req"),
        P("req", None),
        P(None, "seq"),
        P("seq", None),
        P(),
    )
    return jax.shard_map(
        on_device,
        mesh=mesh,
        in_specs=placed,
        out_specs=(P("req", "seq", "cfg"), P("req", "seq", "cfg"), P("req"), P("req")),
        check_vma=False,
    )
```

```python
import math

import jax
import jax.numpy as jnp
from jax import lax
from jax.sharding import PartitionSpec as P


D = 1536
HD = 64
PATCHC = 64
IMG = 512
STEPS = 28


SIGMA_SHIFT = 3.0
GUIDANCE = 5.0
EPSILON = 1e-06
MASKED_SCORE = -1e30


def xor_pairs(axis, distance):
    return [(source, source ^ distance) for source in range(lax.axis_size(axis))]


def shifted(fraction):
    return SIGMA_SHIFT * fraction / (1.0 + (SIGMA_SHIFT - 1.0) * fraction)


def plan(timestep):
    position = timestep.astype(jnp.float32)
    return (shifted(1.0 - position / STEPS), shifted(1.0 - (position + 1.0) / STEPS))


def time_features(sigma):
    half_width = D // 2
    frequency = jnp.exp(-math.log(10000.0) * jnp.arange(half_width, dtype=jnp.float32) / half_width)
    angles = (1000.0 * sigma)[:, None] * frequency[None, :]
    return jnp.concatenate([jnp.cos(angles), jnp.sin(angles)], axis=1)


def layer_norm(values):
    average = jnp.mean(values, axis=-1, keepdims=True)
    centred = values - average
    spread = jnp.mean(centred * centred, axis=-1, keepdims=True)
    return centred * lax.rsqrt(spread + EPSILON)


def gather_by_a2a(value, axis):
    count = lax.axis_size(axis)
    copies = jnp.broadcast_to(value[None], (count,) + value.shape)
    return lax.all_to_all(copies, axis, 0, 0, tiled=True)


def ring_gather(value, axis):
    count = lax.axis_size(axis)
    up = [(source, (source + 1) % count) for source in range(count)]
    down = [(source, (source - 1) % count) for source in range(count)]
    ahead = {0: value}
    from_below, from_above = value, value
    for step in range(1, count // 2 + 1):
        from_below = lax.ppermute(from_below, axis, up)
        ahead[count - step] = from_below
        if step < count - step:
            from_above = lax.ppermute(from_above, axis, down)
            ahead[step] = from_above
    return jnp.stack([ahead[k] for k in range(count)])


def attention(queries, key_rows, value_rows, live_keys):
    scale_factor = HD ** (-0.5)
    scores = (
        jnp.einsum("qhd,khd->hqk", queries, key_rows, preferred_element_type=jnp.float32)
        * scale_factor
    )
    scores = jnp.where(live_keys[None, None, :], scores, MASKED_SCORE)
    highest = jnp.max(scores, axis=-1, keepdims=True)
    exp_scores = jnp.exp(scores - highest)
    weights = (exp_scores / jnp.sum(exp_scores, axis=-1, keepdims=True)).astype(jnp.bfloat16)
    mixture = jnp.einsum("hqk,khd->qhd", weights, value_rows, preferred_element_type=jnp.float32)
    return mixture.astype(jnp.bfloat16)


def on_device(
    img_hidden,
    txt_hidden,
    text_len,
    pooled,
    timestep,
    latent,
    mod_weight,
    mod_bias,
    img_qkv,
    txt_kv,
    out_weight,
    fc_in,
    fc_out,
    final_weight,
):
    group_size = img_hidden.shape[1]
    req_count = lax.axis_size("req")
    seq_count = lax.axis_size("seq")
    half_index = lax.axis_index("cfg")
    cond_first = half_index == 0
    split_rows = out_weight.shape[0] // 2
    own_part = lax.dynamic_slice_in_dim(out_weight, half_index * split_rows, split_rows, 0)
    gathered_part = ring_gather(own_part, "req")
    partner_part = lax.ppermute(gathered_part, "cfg", xor_pairs("cfg", 1))
    every_weight = jnp.concatenate(
        [
            jnp.where(cond_first, gathered_part, partner_part),
            jnp.where(cond_first, partner_part, gathered_part),
        ],
        axis=1,
    )
    half_values = latent.shape[2]
    partner_latent = lax.ppermute(latent, "cfg", xor_pairs("cfg", 1))
    full_latent = jnp.concatenate(
        [
            jnp.where(cond_first, latent, partner_latent),
            jnp.where(cond_first, partner_latent, latent),
        ],
        axis=2,
    )
    current, upcoming = plan(timestep)
    activated = jax.nn.silu(pooled[0] + time_features(current)).astype(jnp.bfloat16)
    columns = jnp.dot(activated, mod_weight, preferred_element_type=jnp.float32) + mod_bias
    block_width = columns.shape[1]
    copies = jnp.broadcast_to(
        columns.reshape(req_count, 1, group_size, block_width),
        (req_count, seq_count, group_size, block_width),
    ).reshape(req_count * seq_count, group_size, block_width)
    every = lax.all_to_all(copies, ("req", "seq"), 0, 0, tiled=True)
    every = every.transpose(1, 0, 2).reshape(group_size, req_count * seq_count * block_width)
    modulation = every.reshape(group_size, 10, 1, D)
    shift_attn, scale_attn, gate_attn = (modulation[:, 0], modulation[:, 1], modulation[:, 2])
    shift_mlp, scale_mlp, gate_mlp = (modulation[:, 3], modulation[:, 4], modulation[:, 5])
    shift_text, scale_text = (modulation[:, 6], modulation[:, 7])
    scale_final, shift_final = (modulation[:, 8], modulation[:, 9])
    img_float = img_hidden[0].astype(jnp.float32)
    img_in = (layer_norm(img_float) * (1.0 + scale_attn) + shift_attn).astype(jnp.bfloat16)
    txt_in = (
        layer_norm(txt_hidden[0].astype(jnp.float32)) * (1.0 + scale_text) + shift_text
    ).astype(jnp.bfloat16)
    row_count = img_in.shape[1]
    text_block = txt_in.shape[1]
    both = ring_gather(jnp.concatenate([img_in, txt_in], axis=1), "req")
    both = both.reshape(req_count * group_size, row_count + text_block, D)
    head_width = img_qkv.shape[2]
    local_heads = head_width // HD
    qkv_columns = img_qkv.reshape(D, 3 * head_width)
    kv_columns = txt_kv.reshape(D, 2 * head_width)
    proj_img = jnp.einsum(
        "rnd,dc->rnc", both[:, :row_count], qkv_columns, preferred_element_type=jnp.float32
    ).astype(jnp.bfloat16)
    proj_txt = jnp.einsum(
        "rnd,dc->rnc", both[:, row_count:], kv_columns, preferred_element_type=jnp.float32
    ).astype(jnp.bfloat16)
    request_count = proj_img.shape[0]
    img_size = row_count * 3 * head_width
    packed = jnp.concatenate(
        [proj_img.reshape(request_count, img_size), proj_txt.reshape(request_count, -1)], axis=1
    )
    packed = jnp.roll(packed, lax.axis_index("req") * group_size, axis=0)
    packed_width = packed.shape[1]
    own = lax.all_to_all(
        packed.reshape(request_count, packed_width // 128, 128), "seq", 0, 0, tiled=True
    ).reshape(request_count, packed_width)
    image_rows = seq_count * row_count
    text_rows = seq_count * text_block
    own_img = own[:, :img_size].reshape(image_rows, 3 * head_width)
    own_txt = own[:, img_size:].reshape(text_rows, 2 * head_width)
    queries = own_img[:, :head_width]
    key_rows = jnp.concatenate([own_img[:, head_width : 2 * head_width], own_txt[:, :head_width]], 0)
    value_rows = jnp.concatenate([own_img[:, 2 * head_width :], own_txt[:, head_width:]], 0)
    text_count = lax.dynamic_index_in_dim(text_len[0], lax.axis_index("seq"), 0, False)
    total_keys = image_rows + text_rows
    live_keys = jnp.arange(total_keys, dtype=jnp.int32) < image_rows + text_count
    attended = attention(
        queries.reshape(image_rows, local_heads, HD),
        key_rows.reshape(total_keys, local_heads, HD),
        value_rows.reshape(total_keys, local_heads, HD),
        live_keys,
    ).reshape(seq_count, row_count, head_width)
    attended_rows = lax.all_to_all(attended, "seq", 0, 0, tiled=True)
    head_columns = lax.all_to_all(
        attended_rows.reshape(req_count, group_size, row_count, head_width), "req", 0, 0, tiled=True
    )
    head_columns = jnp.roll(head_columns, -lax.axis_index("req"), axis=0)
    attn_out = jnp.einsum(
        "grnk,gkd->rnd", head_columns, every_weight, preferred_element_type=jnp.float32
    )
    img_mid = img_float + gate_attn * attn_out
    mlp_in = (layer_norm(img_mid) * (1.0 + scale_mlp) + shift_mlp).astype(jnp.bfloat16)
    all_rows = gather_by_a2a(mlp_in, "seq")
    raised = jnp.einsum("srnd,df->srnf", all_rows, fc_in, preferred_element_type=jnp.float32)
    hidden = jax.nn.gelu(raised, approximate=True).astype(jnp.bfloat16)
    mlp_terms = jnp.einsum(
        "srnf,fd->srnd", hidden, fc_out, preferred_element_type=jnp.float32
    ).astype(jnp.bfloat16)
    block_terms = lax.all_to_all(mlp_terms, "seq", 0, 0, tiled=True)
    mlp_out = jnp.sum(block_terms.astype(jnp.float32), axis=0)
    img_out = img_mid + gate_mlp * mlp_out
    final_in = (layer_norm(img_out) * (1.0 + scale_final) + shift_final).astype(jnp.bfloat16)
    own_velocity = jnp.einsum(
        "rnd,dc->rnc", final_in, final_weight, preferred_element_type=jnp.float32
    )
    other_velocity = lax.ppermute(own_velocity, "cfg", xor_pairs("cfg", 1))
    conditional = jnp.where(cond_first, own_velocity, other_velocity)
    unconditional = jnp.where(cond_first, other_velocity, own_velocity)
    guided = unconditional + GUIDANCE * (conditional - unconditional)
    offset = lax.axis_index("req") * group_size
    step_size = lax.dynamic_slice_in_dim(upcoming - current, offset, group_size, 0)
    next_latent = full_latent + step_size[:, None, None] * guided
    squares = jnp.sum(next_latent * next_latent, axis=(1, 2))
    largest = jnp.max(jnp.abs(next_latent), axis=(1, 2))
    stats = gather_by_a2a(jnp.stack([squares, largest]), "seq")
    squares = jnp.sum(stats[:, 0], axis=0)
    largest = jnp.max(stats[:, 1], axis=0)
    guided = lax.dynamic_slice_in_dim(guided, half_index * half_values, half_values, 2)
    next_latent = lax.dynamic_slice_in_dim(next_latent, half_index * half_values, half_values, 2)
    latent_norm = jnp.sqrt(squares / (IMG * PATCHC))
    return (guided, next_latent, latent_norm, largest)


def solution(mesh):
    placed = (
        P("cfg", "req", "seq", None),
        P("cfg", "req", "seq", None),
        P("cfg", None),
        P("cfg", None, None),
        P(),
        P("req", "seq", "cfg"),
        P(None, ("req", "seq")),
        P(("req", "seq")),
        P(None, None, "req"),
        P(None, None, "req"),
        P("req", None),
        P(None, "seq"),
        P("seq", None),
        P(),
    )
    return jax.shard_map(
        on_device,
        mesh=mesh,
        in_specs=placed,
        out_specs=(P("req", "seq", "cfg"), P("req", "seq", "cfg"), P("req"), P("req")),
        check_vma=False,
    )
```

```python
import math

import jax
import jax.numpy as jnp
from jax import lax
from jax.sharding import PartitionSpec as P


D = 1536
HD = 64
PATCHC = 64
IMG = 512
STEPS = 28


SIGMA_SHIFT = 3.0
GUIDANCE = 5.0
EPSILON = 1e-06
MASKED_SCORE = -1e30


def xor_pairs(axis, distance):
    return [(source, source ^ distance) for source in range(lax.axis_size(axis))]


def shifted(fraction):
    return SIGMA_SHIFT * fraction / (1.0 + (SIGMA_SHIFT - 1.0) * fraction)


def plan(timestep):
    position = timestep.astype(jnp.float32)
    return (shifted(1.0 - position / STEPS), shifted(1.0 - (position + 1.0) / STEPS))


def time_features(sigma):
    half_width = D // 2
    frequency = jnp.exp(-math.log(10000.0) * jnp.arange(half_width, dtype=jnp.float32) / half_width)
    angles = (1000.0 * sigma)[:, None] * frequency[None, :]
    return jnp.concatenate([jnp.cos(angles), jnp.sin(angles)], axis=1)


def layer_norm(values):
    average = jnp.mean(values, axis=-1, keepdims=True)
    centred = values - average
    spread = jnp.mean(centred * centred, axis=-1, keepdims=True)
    return centred * lax.rsqrt(spread + EPSILON)


def gather_by_a2a(value, axis):
    count = lax.axis_size(axis)
    copies = jnp.broadcast_to(value[None], (count,) + value.shape)
    return lax.all_to_all(copies, axis, 0, 0, tiled=True)


def ring_gather(value, axis):
    count = lax.axis_size(axis)
    up = [(source, (source + 1) % count) for source in range(count)]
    down = [(source, (source - 1) % count) for source in range(count)]
    ahead = {0: value}
    from_below, from_above = value, value
    for step in range(1, count // 2 + 1):
        from_below = lax.ppermute(from_below, axis, up)
        ahead[count - step] = from_below
        if step < count - step:
            from_above = lax.ppermute(from_above, axis, down)
            ahead[step] = from_above
    return jnp.stack([ahead[k] for k in range(count)])


def attention(queries, key_rows, value_rows, live_keys):
    scale_factor = HD ** (-0.5)
    scores = (
        jnp.einsum("qhd,khd->hqk", queries, key_rows, preferred_element_type=jnp.float32)
        * scale_factor
    )
    scores = jnp.where(live_keys[None, None, :], scores, MASKED_SCORE)
    highest = jnp.max(scores, axis=-1, keepdims=True)
    exp_scores = jnp.exp(scores - highest)
    weights = (exp_scores / jnp.sum(exp_scores, axis=-1, keepdims=True)).astype(jnp.bfloat16)
    mixture = jnp.einsum("hqk,khd->qhd", weights, value_rows, preferred_element_type=jnp.float32)
    return mixture.astype(jnp.bfloat16)


def on_device(
    img_hidden,
    txt_hidden,
    text_len,
    pooled,
    timestep,
    latent,
    mod_weight,
    mod_bias,
    img_qkv,
    txt_kv,
    out_weight,
    fc_in,
    fc_out,
    final_weight,
):
    group_size = img_hidden.shape[1]
    req_count = lax.axis_size("req")
    seq_count = lax.axis_size("seq")
    half_index = lax.axis_index("cfg")
    cond_first = half_index == 0
    split_rows = out_weight.shape[0] // 2
    own_part = lax.dynamic_slice_in_dim(out_weight, half_index * split_rows, split_rows, 0)
    gathered_part = ring_gather(own_part, "req")
    partner_part = lax.ppermute(gathered_part, "cfg", xor_pairs("cfg", 1))
    every_weight = jnp.concatenate(
        [
            jnp.where(cond_first, gathered_part, partner_part),
            jnp.where(cond_first, partner_part, gathered_part),
        ],
        axis=1,
    )
    half_values = latent.shape[2]
    partner_latent = lax.ppermute(latent, "cfg", xor_pairs("cfg", 1))
    full_latent = jnp.concatenate(
        [
            jnp.where(cond_first, latent, partner_latent),
            jnp.where(cond_first, partner_latent, latent),
        ],
        axis=2,
    )
    current, upcoming = plan(timestep)
    activated = jax.nn.silu(pooled[0] + time_features(current)).astype(jnp.bfloat16)
    columns = jnp.dot(activated, mod_weight, preferred_element_type=jnp.float32) + mod_bias
    block_width = columns.shape[1]
    copies = jnp.broadcast_to(
        columns.reshape(req_count, 1, group_size, block_width),
        (req_count, seq_count, group_size, block_width),
    ).reshape(req_count * seq_count, group_size, block_width)
    every = lax.all_to_all(copies, ("req", "seq"), 0, 0, tiled=True)
    every = every.transpose(1, 0, 2).reshape(group_size, req_count * seq_count * block_width)
    modulation = every.reshape(group_size, 10, 1, D)
    shift_attn, scale_attn, gate_attn = (modulation[:, 0], modulation[:, 1], modulation[:, 2])
    shift_mlp, scale_mlp, gate_mlp = (modulation[:, 3], modulation[:, 4], modulation[:, 5])
    shift_text, scale_text = (modulation[:, 6], modulation[:, 7])
    scale_final, shift_final = (modulation[:, 8], modulation[:, 9])
    img_float = img_hidden[0].astype(jnp.float32)
    img_in = (layer_norm(img_float) * (1.0 + scale_attn) + shift_attn).astype(jnp.bfloat16)
    txt_in = (
        layer_norm(txt_hidden[0].astype(jnp.float32)) * (1.0 + scale_text) + shift_text
    ).astype(jnp.bfloat16)
    row_count = img_in.shape[1]
    text_block = txt_in.shape[1]
    both = ring_gather(jnp.concatenate([img_in, txt_in], axis=1), "req")
    both = both.reshape(req_count * group_size, row_count + text_block, D)
    head_width = img_qkv.shape[2]
    local_heads = head_width // HD
    qkv_columns = img_qkv.reshape(D, 3 * head_width)
    kv_columns = txt_kv.reshape(D, 2 * head_width)
    proj_img = jnp.einsum(
        "rnd,dc->rnc", both[:, :row_count], qkv_columns, preferred_element_type=jnp.float32
    ).astype(jnp.bfloat16)
    proj_txt = jnp.einsum(
        "rnd,dc->rnc", both[:, row_count:], kv_columns, preferred_element_type=jnp.float32
    ).astype(jnp.bfloat16)
    request_count = proj_img.shape[0]
    img_size = row_count * 3 * head_width
    packed = jnp.concatenate(
        [proj_img.reshape(request_count, img_size), proj_txt.reshape(request_count, -1)], axis=1
    )
    packed = jnp.roll(packed, lax.axis_index("req") * group_size, axis=0)
    packed_width = packed.shape[1]
    own = lax.all_to_all(
        packed.reshape(request_count, packed_width // 128, 128), "seq", 0, 0, tiled=True
    ).reshape(request_count, packed_width)
    image_rows = seq_count * row_count
    text_rows = seq_count * text_block
    own_img = own[:, :img_size].reshape(image_rows, 3 * head_width)
    own_txt = own[:, img_size:].reshape(text_rows, 2 * head_width)
    queries = own_img[:, :head_width]
    key_rows = jnp.concatenate([own_img[:, head_width : 2 * head_width], own_txt[:, :head_width]], 0)
    value_rows = jnp.concatenate([own_img[:, 2 * head_width :], own_txt[:, head_width:]], 0)
    text_count = lax.dynamic_index_in_dim(text_len[0], lax.axis_index("seq"), 0, False)
    total_keys = image_rows + text_rows
    live_keys = jnp.arange(total_keys, dtype=jnp.int32) < image_rows + text_count
    attended = attention(
        queries.reshape(image_rows, local_heads, HD),
        key_rows.reshape(total_keys, local_heads, HD),
        value_rows.reshape(total_keys, local_heads, HD),
        live_keys,
    ).reshape(seq_count, row_count, head_width)
    attended_rows = lax.all_to_all(
        attended.reshape(seq_count, row_count * head_width // 128, 128), "seq", 0, 0, tiled=True
    ).reshape(seq_count, row_count, head_width)
    head_columns = lax.all_to_all(
        attended_rows.reshape(req_count, group_size * row_count * head_width // 128, 128),
        "req",
        0,
        0,
        tiled=True,
    ).reshape(req_count, group_size, row_count, head_width)
    head_columns = jnp.roll(head_columns, -lax.axis_index("req"), axis=0)
    attn_out = jnp.einsum(
        "grnk,gkd->rnd", head_columns, every_weight, preferred_element_type=jnp.float32
    )
    img_mid = img_float + gate_attn * attn_out
    mlp_in = (layer_norm(img_mid) * (1.0 + scale_mlp) + shift_mlp).astype(jnp.bfloat16)
    all_rows = gather_by_a2a(mlp_in, "seq")
    raised = jnp.einsum("srnd,df->srnf", all_rows, fc_in, preferred_element_type=jnp.float32)
    hidden = jax.nn.gelu(raised, approximate=True).astype(jnp.bfloat16)
    mlp_terms = jnp.einsum(
        "srnf,fd->srnd", hidden, fc_out, preferred_element_type=jnp.float32
    ).astype(jnp.bfloat16)
    block_terms = lax.all_to_all(mlp_terms, "seq", 0, 0, tiled=True)
    mlp_out = jnp.sum(block_terms.astype(jnp.float32), axis=0)
    img_out = img_mid + gate_mlp * mlp_out
    final_in = (layer_norm(img_out) * (1.0 + scale_final) + shift_final).astype(jnp.bfloat16)
    own_velocity = jnp.einsum(
        "rnd,dc->rnc", final_in, final_weight, preferred_element_type=jnp.float32
    )
    other_velocity = lax.ppermute(own_velocity, "cfg", xor_pairs("cfg", 1))
    conditional = jnp.where(cond_first, own_velocity, other_velocity)
    unconditional = jnp.where(cond_first, other_velocity, own_velocity)
    guided = unconditional + GUIDANCE * (conditional - unconditional)
    offset = lax.axis_index("req") * group_size
    step_size = lax.dynamic_slice_in_dim(upcoming - current, offset, group_size, 0)
    next_latent = full_latent + step_size[:, None, None] * guided
    squares = jnp.sum(next_latent * next_latent, axis=(1, 2))
    largest = jnp.max(jnp.abs(next_latent), axis=(1, 2))
    stats = gather_by_a2a(jnp.stack([squares, largest]), "seq")
    squares = jnp.sum(stats[:, 0], axis=0)
    largest = jnp.max(stats[:, 1], axis=0)
    guided = lax.dynamic_slice_in_dim(guided, half_index * half_values, half_values, 2)
    next_latent = lax.dynamic_slice_in_dim(next_latent, half_index * half_values, half_values, 2)
    latent_norm = jnp.sqrt(squares / (IMG * PATCHC))
    return (guided, next_latent, latent_norm, largest)


def solution(mesh):
    placed = (
        P("cfg", "req", "seq", None),
        P("cfg", "req", "seq", None),
        P("cfg", None),
        P("cfg", None, None),
        P(),
        P("req", "seq", "cfg"),
        P(None, ("req", "seq")),
        P(("req", "seq")),
        P(None, None, "req"),
        P(None, None, "req"),
        P("req", None),
        P(None, "seq"),
        P("seq", None),
        P(),
    )
    return jax.shard_map(
        on_device,
        mesh=mesh,
        in_specs=placed,
        out_specs=(P("req", "seq", "cfg"), P("req", "seq", "cfg"), P("req"), P("req")),
        check_vma=False,
    )
```

```python
import math

import jax
import jax.numpy as jnp
from jax import lax
from jax.sharding import PartitionSpec as P


D = 1536
HD = 64
PATCHC = 64
IMG = 512
STEPS = 28


SIGMA_SHIFT = 3.0
GUIDANCE = 5.0
EPSILON = 1e-06
MASKED_SCORE = -1e30


def xor_pairs(axis, distance):
    return [(source, source ^ distance) for source in range(lax.axis_size(axis))]


def shifted(fraction):
    return SIGMA_SHIFT * fraction / (1.0 + (SIGMA_SHIFT - 1.0) * fraction)


def plan(timestep):
    position = timestep.astype(jnp.float32)
    return (shifted(1.0 - position / STEPS), shifted(1.0 - (position + 1.0) / STEPS))


def time_features(sigma):
    half_width = D // 2
    frequency = jnp.exp(-math.log(10000.0) * jnp.arange(half_width, dtype=jnp.float32) / half_width)
    angles = (1000.0 * sigma)[:, None] * frequency[None, :]
    return jnp.concatenate([jnp.cos(angles), jnp.sin(angles)], axis=1)


def layer_norm(values):
    average = jnp.mean(values, axis=-1, keepdims=True)
    centred = values - average
    spread = jnp.mean(centred * centred, axis=-1, keepdims=True)
    return centred * lax.rsqrt(spread + EPSILON)


def gather_by_a2a(value, axis):
    count = lax.axis_size(axis)
    copies = jnp.broadcast_to(value[None], (count,) + value.shape)
    return lax.all_to_all(copies, axis, 0, 0, tiled=True)


def ring_gather(value, axis):
    count = lax.axis_size(axis)
    up = [(source, (source + 1) % count) for source in range(count)]
    down = [(source, (source - 1) % count) for source in range(count)]
    ahead = {0: value}
    from_below, from_above = value, value
    for step in range(1, count // 2 + 1):
        from_below = lax.ppermute(from_below, axis, up)
        ahead[count - step] = from_below
        if step < count - step:
            from_above = lax.ppermute(from_above, axis, down)
            ahead[step] = from_above
    return jnp.stack([ahead[k] for k in range(count)])


def attention(queries, key_rows, value_rows, live_keys):
    scale_factor = HD ** (-0.5)
    scores = (
        jnp.einsum("qhd,khd->hqk", queries, key_rows, preferred_element_type=jnp.float32)
        * scale_factor
    )
    scores = jnp.where(live_keys[None, None, :], scores, MASKED_SCORE)
    highest = jnp.max(scores, axis=-1, keepdims=True)
    exp_scores = jnp.exp(scores - highest)
    weights = (exp_scores / jnp.sum(exp_scores, axis=-1, keepdims=True)).astype(jnp.bfloat16)
    mixture = jnp.einsum("hqk,khd->qhd", weights, value_rows, preferred_element_type=jnp.float32)
    return mixture.astype(jnp.bfloat16)


def on_device(
    img_hidden,
    txt_hidden,
    text_len,
    pooled,
    timestep,
    latent,
    mod_weight,
    mod_bias,
    img_qkv,
    txt_kv,
    out_weight,
    fc_in,
    fc_out,
    final_weight,
):
    group_size = img_hidden.shape[1]
    req_count = lax.axis_size("req")
    seq_count = lax.axis_size("seq")
    half_index = lax.axis_index("cfg")
    cond_first = half_index == 0
    split_rows = out_weight.shape[0] // 2
    own_part = lax.dynamic_slice_in_dim(out_weight, half_index * split_rows, split_rows, 0)
    gathered_part = ring_gather(own_part, "req")
    partner_part = lax.ppermute(gathered_part, "cfg", xor_pairs("cfg", 1))
    every_weight = jnp.concatenate(
        [
            jnp.where(cond_first, gathered_part, partner_part),
            jnp.where(cond_first, partner_part, gathered_part),
        ],
        axis=1,
    )
    half_values = latent.shape[2]
    partner_latent = lax.ppermute(latent, "cfg", xor_pairs("cfg", 1))
    full_latent = jnp.concatenate(
        [
            jnp.where(cond_first, latent, partner_latent),
            jnp.where(cond_first, partner_latent, latent),
        ],
        axis=2,
    )
    current, upcoming = plan(timestep)
    activated = jax.nn.silu(pooled[0] + time_features(current)).astype(jnp.bfloat16)
    columns = jnp.dot(activated, mod_weight, preferred_element_type=jnp.float32) + mod_bias
    block_width = columns.shape[1]
    lane_width = -(-block_width // 128) * 128
    padded = jnp.pad(columns, ((0, 0), (0, lane_width - block_width)))
    copies = jnp.broadcast_to(
        padded.reshape(req_count, 1, group_size, lane_width),
        (req_count, seq_count, group_size, lane_width),
    ).reshape(req_count * seq_count, group_size, lane_width)
    every = lax.all_to_all(copies, ("req", "seq"), 0, 0, tiled=True)
    every = every[:, :, :block_width].transpose(1, 0, 2)
    every = every.reshape(group_size, req_count * seq_count * block_width)
    modulation = every.reshape(group_size, 10, 1, D)
    shift_attn, scale_attn, gate_attn = (modulation[:, 0], modulation[:, 1], modulation[:, 2])
    shift_mlp, scale_mlp, gate_mlp = (modulation[:, 3], modulation[:, 4], modulation[:, 5])
    shift_text, scale_text = (modulation[:, 6], modulation[:, 7])
    scale_final, shift_final = (modulation[:, 8], modulation[:, 9])
    img_float = img_hidden[0].astype(jnp.float32)
    img_in = (layer_norm(img_float) * (1.0 + scale_attn) + shift_attn).astype(jnp.bfloat16)
    txt_in = (
        layer_norm(txt_hidden[0].astype(jnp.float32)) * (1.0 + scale_text) + shift_text
    ).astype(jnp.bfloat16)
    row_count = img_in.shape[1]
    text_block = txt_in.shape[1]
    rows_in = jnp.concatenate([img_in, txt_in], axis=1)
    both = ring_gather(rows_in.reshape(-1, 128), "req").reshape((req_count,) + rows_in.shape)
    both = both.reshape(req_count * group_size, row_count + text_block, D)
    head_width = img_qkv.shape[2]
    local_heads = head_width // HD
    qkv_columns = img_qkv.reshape(D, 3 * head_width)
    kv_columns = txt_kv.reshape(D, 2 * head_width)
    proj_img = jnp.einsum(
        "rnd,dc->rnc", both[:, :row_count], qkv_columns, preferred_element_type=jnp.float32
    ).astype(jnp.bfloat16)
    proj_txt = jnp.einsum(
        "rnd,dc->rnc", both[:, row_count:], kv_columns, preferred_element_type=jnp.float32
    ).astype(jnp.bfloat16)
    request_count = proj_img.shape[0]
    img_size = row_count * 3 * head_width
    packed = jnp.concatenate(
        [proj_img.reshape(request_count, img_size), proj_txt.reshape(request_count, -1)], axis=1
    )
    packed = jnp.roll(packed, lax.axis_index("req") * group_size, axis=0)
    packed_width = packed.shape[1]
    own = lax.all_to_all(
        packed.reshape(request_count, packed_width // 128, 128), "seq", 0, 0, tiled=True
    ).reshape(request_count, packed_width)
    image_rows = seq_count * row_count
    text_rows = seq_count * text_block
    own_img = own[:, :img_size].reshape(image_rows, 3 * head_width)
    own_txt = own[:, img_size:].reshape(text_rows, 2 * head_width)
    queries = own_img[:, :head_width]
    key_rows = jnp.concatenate([own_img[:, head_width : 2 * head_width], own_txt[:, :head_width]], 0)
    value_rows = jnp.concatenate([own_img[:, 2 * head_width :], own_txt[:, head_width:]], 0)
    text_count = lax.dynamic_index_in_dim(text_len[0], lax.axis_index("seq"), 0, False)
    total_keys = image_rows + text_rows
    live_keys = jnp.arange(total_keys, dtype=jnp.int32) < image_rows + text_count
    attended = attention(
        queries.reshape(image_rows, local_heads, HD),
        key_rows.reshape(total_keys, local_heads, HD),
        value_rows.reshape(total_keys, local_heads, HD),
        live_keys,
    ).reshape(seq_count, row_count, head_width)
    attended_rows = lax.all_to_all(
        attended.reshape(seq_count, row_count * head_width // 128, 128), "seq", 0, 0, tiled=True
    ).reshape(seq_count, row_count, head_width)
    head_columns = lax.all_to_all(
        attended_rows.reshape(req_count, group_size * row_count * head_width // 128, 128),
        "req",
        0,
        0,
        tiled=True,
    ).reshape(req_count, group_size, row_count, head_width)
    head_columns = jnp.roll(head_columns, -lax.axis_index("req"), axis=0)
    attn_out = jnp.einsum(
        "grnk,gkd->rnd", head_columns, every_weight, preferred_element_type=jnp.float32
    )
    img_mid = img_float + gate_attn * attn_out
    mlp_in = (layer_norm(img_mid) * (1.0 + scale_mlp) + shift_mlp).astype(jnp.bfloat16)
    all_rows = gather_by_a2a(mlp_in, "seq")
    raised = jnp.einsum("srnd,df->srnf", all_rows, fc_in, preferred_element_type=jnp.float32)
    hidden = jax.nn.gelu(raised, approximate=True).astype(jnp.bfloat16)
    mlp_terms = jnp.einsum(
        "srnf,fd->srnd", hidden, fc_out, preferred_element_type=jnp.float32
    ).astype(jnp.bfloat16)
    block_terms = lax.all_to_all(mlp_terms, "seq", 0, 0, tiled=True)
    mlp_out = jnp.sum(block_terms.astype(jnp.float32), axis=0)
    img_out = img_mid + gate_mlp * mlp_out
    final_in = (layer_norm(img_out) * (1.0 + scale_final) + shift_final).astype(jnp.bfloat16)
    own_velocity = jnp.einsum(
        "rnd,dc->rnc", final_in, final_weight, preferred_element_type=jnp.float32
    )
    other_velocity = lax.ppermute(own_velocity, "cfg", xor_pairs("cfg", 1))
    conditional = jnp.where(cond_first, own_velocity, other_velocity)
    unconditional = jnp.where(cond_first, other_velocity, own_velocity)
    guided = unconditional + GUIDANCE * (conditional - unconditional)
    offset = lax.axis_index("req") * group_size
    step_size = lax.dynamic_slice_in_dim(upcoming - current, offset, group_size, 0)
    next_latent = full_latent + step_size[:, None, None] * guided
    squares = jnp.sum(next_latent * next_latent, axis=(1, 2))
    largest = jnp.max(jnp.abs(next_latent), axis=(1, 2))
    stats = gather_by_a2a(jnp.stack([squares, largest]), "seq")
    squares = jnp.sum(stats[:, 0], axis=0)
    largest = jnp.max(stats[:, 1], axis=0)
    guided = lax.dynamic_slice_in_dim(guided, half_index * half_values, half_values, 2)
    next_latent = lax.dynamic_slice_in_dim(next_latent, half_index * half_values, half_values, 2)
    latent_norm = jnp.sqrt(squares / (IMG * PATCHC))
    return (guided, next_latent, latent_norm, largest)


def solution(mesh):
    placed = (
        P("cfg", "req", "seq", None),
        P("cfg", "req", "seq", None),
        P("cfg", None),
        P("cfg", None, None),
        P(),
        P("req", "seq", "cfg"),
        P(None, ("req", "seq")),
        P(("req", "seq")),
        P(None, None, "req"),
        P(None, None, "req"),
        P("req", None),
        P(None, "seq"),
        P("seq", None),
        P(),
    )
    return jax.shard_map(
        on_device,
        mesh=mesh,
        in_specs=placed,
        out_specs=(P("req", "seq", "cfg"), P("req", "seq", "cfg"), P("req"), P("req")),
        check_vma=False,
    )
```
